256 devices in a mesh: gx: 8 (over y, core), gy: 32 (over z, x).
Axes of the slice: x: 4, y: 4, z: 8, core: 2. Of those that a mesh axis runs over, the one named last changes fastest.
Arguments:
- source_field: float32 [4096, 64, 256], P('gx', 'gy'), may hold values from -6 to 6
- permeability: float32 [4096, 64, 256], P('gx', 'gy'), may hold values from 0.3 to 3
- layer_ids: int32 [256], replicated, may hold values from 0 to 3, as said below
- inverse_fine: float32 [4, 4096, 512], P(None, 'gx'), as said below
- couple_fine: float32 [2, 4, 8], P(None, None, 'gx'), may hold values from 0.35 to 0.7
- inverse_coarse: float32 [4, 4096, 512], P(None, 'gx'), as said below
- couple_coarse: float32 [2, 4, 8], P(None, None, 'gx'), may hold values from 0.35 to 0.7
- owner_map: int32 [32, 1], replicated, may hold values from 0 to 7
Outputs:
- solution_fine: float32 [4096, 64, 256], P('gx', 'gy')
- residual_fine: float32 [4096, 64, 256], P('gx', 'gy')
- solution_coarse: float32 [4096, 32, 256], P('gx', 'gy')
The draws below stay inside these ranges and needn't reach their ends.
Inputs may be any that keep to these rules, and one draw needn't show every extreme that they name: owner_map names the aggregate of each level-6 plane; every aggregate below 8 holds at least one plane. `layer_ids`: every rock type names the same number of z cells. `inverse_fine`: each block is a positive-definite dense matrix with a diagonal dominating each line solve's coupling. `inverse_coarse`: each block is a positive-definite dense matrix with a diagonal dominating each line solve's coupling.
All inputs are finite; a program needn't handle non-finite values.
Results may differ from the reference program's by a relative error of at most 0.00012.
Values sent between devices are 32-bit elements; how exact they have to be, the bound alone decides.
No kernel may reach another device: no remote copies, remote signals or barrier semaphores. Data moves between devices by JAX's collectives and lax.ppermute only.
A program may use at most 128 MiB of HBM per device.

```python
import math
import jax
import jax.numpy as jnp
from jax import lax

CX = 512
NZ = 256
NL = 4
NSWEEP = 3
NX = 4096
NY5 = 64
NY6 = 32
NAGG = 8
N_GX = 8


def make_inverse(base_key):
    diag_key, noise_key = jax.random.split(base_key)
    row_index = jnp.arange(NX) % CX
    col_index = jnp.arange(CX)
    distance = jnp.abs(row_index[:, None] - col_index[None, :]).astype(jnp.float32)
    identity = (row_index[:, None] == col_index[None, :]).astype(jnp.float32)
    kernel = 0.5 * jnp.exp(-0.6 * distance / CX)
    diagonal = jax.random.uniform(diag_key, (NL, NX, 1), jnp.float32, 0.2, 0.5)
    noise_part = jax.random.uniform(noise_key, (NL, NX, CX), jnp.float32, -1.0, 1.0)
    noise_scale = 0.25 / math.sqrt(CX)
    return kernel[None] + identity[None] * diagonal + noise_scale * noise_part


def draw_inverse_fine(key, part):
    return make_inverse(jax.random.fold_in(key, 11))


def draw_inverse_coarse(key, part):
    return make_inverse(jax.random.fold_in(key, 23))


def draw_layer_ids(key, part):
    shuffled = jax.random.permutation(jax.random.fold_in(key, 37), NZ)
    return (shuffled % NL).astype(jnp.int32)


def block_levels(own_key, shape, shards, least, high):
    gain, own = 1.0, jax.random.fold_in(own_key, 6)
    for axis_at, blocks in shards:
        steps = jnp.exp(jax.random.uniform(jax.random.fold_in(own, axis_at), (blocks,), jnp.float32, least / len(shards), high / len(shards)))
        gain = gain * jnp.repeat(steps, shape[axis_at] // blocks).reshape([-1 if axis == axis_at else 1 for axis in range(len(shape))])
    return gain


def picks_of(stream_key, rows, number_of, top, lift):
    sequence = jax.random.permutation(jax.random.fold_in(stream_key, 1), number_of)
    pull = sequence
    for power in range(3):
        pull = pull * pull // number_of
    pull = pull * lift // number_of
    chance = jax.random.randint(jax.random.fold_in(stream_key, 2), (rows, number_of), 0, 4096) + pull
    sure = jax.random.permutation(jax.random.fold_in(stream_key, 3), rows)[jnp.arange(number_of) % rows]
    chance = jnp.where(jnp.arange(rows)[:, None] == sure[None, :], 1 << 14, chance)
    score = chance * number_of + jnp.arange(number_of)
    return lax.top_k(score.astype(jnp.int32), top)[1].astype(jnp.int32)


def bell_draw(own_key, dims, width, bound, cuts=(), kind=jnp.bfloat16):
    values = width * jax.random.normal(own_key, dims, jnp.float32)
    if cuts:
        values = values * block_levels(own_key, dims, cuts, -0.22, 0.18)
    return jnp.clip(values, -bound, bound).astype(kind)


def setup_inputs(seed: int = 0) -> dict:
    arg_keys = jax.random.split(jax.random.key(seed), 9)
    return {
        "source_field": bell_draw(arg_keys[0], (NX, NY5, NZ), 1.0, 6.0, ((0, 8), (1, 32)), jnp.float32),
        "permeability": jnp.clip(jnp.exp(math.log(3.0) - 2.3025851 * jax.random.uniform(arg_keys[1], (NX, NY5, NZ), jnp.float32) ** block_levels(arg_keys[1], (NX, NY5, NZ), ((0, 8), (1, 32)), -0.2, 0.2)), 0.3, 3.0),
        "layer_ids": draw_layer_ids(jax.random.fold_in(arg_keys[8], 71), 0),
        "inverse_fine": draw_inverse_fine(jax.random.fold_in(arg_keys[8], 71), 0),
        "couple_fine": jnp.clip(0.35 + 0.35 * jax.random.uniform(arg_keys[4], (2, NL, N_GX), jnp.float32) ** block_levels(arg_keys[4], (2, NL, N_GX), ((2, 8),), -0.2, 0.2), 0.35, 0.7),
        "inverse_coarse": draw_inverse_coarse(jax.random.fold_in(arg_keys[8], 71), 0),
        "couple_coarse": jnp.clip(0.35 + 0.35 * jax.random.uniform(arg_keys[6], (2, NL, N_GX), jnp.float32) ** block_levels(arg_keys[6], (2, NL, N_GX), ((2, 8),), -0.2, 0.2), 0.35, 0.7),
        "owner_map": picks_of(arg_keys[7], NY6, NAGG, 1, 1024),
    }


PRECISE = lax.Precision.HIGHEST
WEIGHTS = (0.5, 0.5, 0.15, 0.15, 0.05, 0.05)
STORAGE = 0.1


def neighbours(padded):
    return [padded[:-2, 1:-1, 1:-1], padded[2:, 1:-1, 1:-1], padded[1:-1, :-2, 1:-1],
            padded[1:-1, 2:, 1:-1], padded[1:-1, 1:-1, :-2], padded[1:-1, 1:-1, 2:]]


def face_terms(padded):
    centre = padded[1:-1, 1:-1, 1:-1]
    return [weight * 2.0 * centre * beside / (centre + beside) for weight, beside in zip(WEIGHTS, neighbours(padded))]


def apply_operator(padded, face_list):
    centre = padded[1:-1, 1:-1, 1:-1]
    result_sum = STORAGE * centre
    for face_term, beside in zip(face_list, neighbours(padded)):
        result_sum = result_sum + face_term * (centre - beside)
    return result_sum


def chain_solve(chain_rows):
    blocks_count = chain_rows.shape[0]
    carry_value = jnp.zeros_like(chain_rows[0, 0])
    carry_gain = jnp.zeros_like(chain_rows[0, 0])
    first_parts, first_links, last_parts, last_links = [], [], [], []
    for block_index in range(blocks_count):
        pivot_value = 1.0 - chain_rows[block_index, 2] * carry_gain
        first_part = (chain_rows[block_index, 0] - chain_rows[block_index, 2] * carry_value) / pivot_value
        first_link = chain_rows[block_index, 4] / pivot_value
        carry_value = chain_rows[block_index, 1] - chain_rows[block_index, 3] * carry_value + chain_rows[block_index, 3] * carry_gain * first_part
        carry_gain = chain_rows[block_index, 5] + chain_rows[block_index, 3] * carry_gain * first_link
        first_parts.append(first_part)
        first_links.append(first_link)
        last_parts.append(carry_value)
        last_links.append(carry_gain)
    following = jnp.zeros_like(carry_value)
    last_values = [following] * blocks_count
    next_values = [following] * blocks_count
    for block_index in range(blocks_count - 1, -1, -1):
        next_values[block_index] = following
        last_values[block_index] = last_parts[block_index] - last_links[block_index] * following
        following = first_parts[block_index] - first_links[block_index] * following
    previous = [jnp.zeros_like(following)] + last_values[:-1]
    return jnp.stack([jnp.stack([previous[block_index], next_values[block_index]]) for block_index in range(blocks_count)])


def line_solve(source, inverse, couple, layer_ids):
    blocks_count = couple.shape[2]
    block_width = inverse.shape[2]
    line_count = source.shape[1]
    blocks = inverse.reshape(inverse.shape[0], blocks_count, block_width, block_width)

    def per_depth(depth_index):
        layer_index = layer_ids[depth_index]
        matrix = blocks[layer_index]
        lower_couple = couple[0, layer_index]
        upper_couple = couple[1, layer_index]
        column = lax.dynamic_index_in_dim(source, depth_index, 2, keepdims=False).reshape(blocks_count, block_width, line_count)
        values = jnp.einsum("pic,pcy->piy", matrix, column, precision=PRECISE)
        shaped = (blocks_count, line_count)
        chain_rows = jnp.stack([
            values[:, 0, :], values[:, -1, :],
            jnp.broadcast_to((lower_couple * matrix[:, 0, 0])[:, None], shaped),
            jnp.broadcast_to((lower_couple * matrix[:, -1, 0])[:, None], shaped),
            jnp.broadcast_to((upper_couple * matrix[:, 0, -1])[:, None], shaped),
            jnp.broadcast_to((upper_couple * matrix[:, -1, -1])[:, None], shaped)], axis=1)
        solved = chain_solve(chain_rows)
        result = values - (lower_couple[:, None] * solved[:, 0, :])[:, None, :] * matrix[:, :, 0][:, :, None] \
            - (upper_couple[:, None] * solved[:, 1, :])[:, None, :] * matrix[:, :, -1][:, :, None]
        return result.reshape(blocks_count * block_width, line_count)

    depths = jnp.arange(source.shape[2], dtype=jnp.int32)
    return jnp.transpose(lax.map(per_depth, depths), (1, 2, 0))


def reference(source_field, permeability, layer_ids, inverse_fine, couple_fine, inverse_coarse, couple_coarse, owner_map):
    face_list = face_terms(jnp.pad(permeability, 1))
    solution = jnp.zeros_like(source_field)
    for sweep_index in range(NSWEEP):
        update = source_field - apply_operator(jnp.pad(solution, 1), face_list)
        solution = solution + line_solve(update, inverse_fine, couple_fine, layer_ids)
    residual = source_field - apply_operator(jnp.pad(solution, 1), face_list)
    coarse = 0.5 * (residual[:, 0::2, :] + residual[:, 1::2, :])
    owners = owner_map[:, 0]
    member = (owners[:, None] == jnp.arange(NAGG, dtype=jnp.int32)[None, :]).astype(jnp.float32)
    aggregate = jnp.einsum("xjz,jo->xoz", coarse, member, precision=PRECISE)
    smoothed = line_solve(aggregate, inverse_coarse, couple_coarse, layer_ids)
    solution_coarse = jnp.take(smoothed, owners, axis=1)
    return solution, residual, solution_coarse
```

```python
import jax
import jax.numpy as jnp
from jax import lax
from jax.sharding import PartitionSpec as P

NSWEEP = 3


PRECISE = lax.Precision.HIGHEST
WEIGHTS = (0.5, 0.5, 0.15, 0.15, 0.05, 0.05)
STORAGE = 0.1


def with_halo(array, sides, width):
    for axis, dim in sides:
        peers, length = (lax.axis_size(axis), array.shape[dim])
        up = [(i, (i + 1) % peers) for i in range(peers - 1)]
        down = [(j, i) for i, j in up]
        last = lax.slice_in_dim(array, length - width, length, axis=dim)
        leading = lax.slice_in_dim(array, 0, width, axis=dim)
        before = lax.ppermute(last, axis, up)
        after = lax.ppermute(leading, axis, down)
        array = jnp.concatenate([before, array, after], axis=dim)
    return array


def neighbours(padded):
    return [
        padded[:-2, 1:-1, 1:-1],
        padded[2:, 1:-1, 1:-1],
        padded[1:-1, :-2, 1:-1],
        padded[1:-1, 2:, 1:-1],
        padded[1:-1, 1:-1, :-2],
        padded[1:-1, 1:-1, 2:],
    ]


def face_terms(padded):
    centre = padded[1:-1, 1:-1, 1:-1]
    return [
        weight * 2.0 * centre * beside / (centre + beside)
        for weight, beside in zip(WEIGHTS, neighbours(padded))
    ]


def apply_operator(padded, face_list):
    centre = padded[1:-1, 1:-1, 1:-1]
    result_sum = STORAGE * centre
    for face_term, beside in zip(face_list, neighbours(padded)):
        result_sum = result_sum + face_term * (centre - beside)
    return result_sum


def padded_depth(field_now):
    return jnp.pad(field_now, ((0, 0), (0, 0), (1, 1)))


def chain_solve(chain_rows):
    blocks_count = chain_rows.shape[0]
    carry_value = jnp.zeros_like(chain_rows[0, 0])
    carry_gain = jnp.zeros_like(chain_rows[0, 0])
    first_parts, first_links, last_parts, last_links = ([], [], [], [])
    for block_index in range(blocks_count):
        pivot_value = 1.0 - chain_rows[block_index, 2] * carry_gain
        first_part = (
            chain_rows[block_index, 0] - chain_rows[block_index, 2] * carry_value
        ) / pivot_value
        first_link = chain_rows[block_index, 4] / pivot_value
        carry_value = (
            chain_rows[block_index, 1]
            - chain_rows[block_index, 3] * carry_value
            + chain_rows[block_index, 3] * carry_gain * first_part
        )
        carry_gain = (
            chain_rows[block_index, 5] + chain_rows[block_index, 3] * carry_gain * first_link
        )
        first_parts.append(first_part)
        first_links.append(first_link)
        last_parts.append(carry_value)
        last_links.append(carry_gain)
    following = jnp.zeros_like(carry_value)
    last_values = [following] * blocks_count
    next_values = [following] * blocks_count
    for block_index in range(blocks_count - 1, -1, -1):
        next_values[block_index] = following
        last_values[block_index] = last_parts[block_index] - last_links[block_index] * following
        following = first_parts[block_index] - first_links[block_index] * following
    previous = [jnp.zeros_like(following)] + last_values[:-1]
    return jnp.stack(
        [
            jnp.stack([previous[block_index], next_values[block_index]])
            for block_index in range(blocks_count)
        ]
    )


def reduced_solve(chain_local):
    packed = chain_local[None]
    everyone = lax.all_gather(packed, "gx", axis=0, tiled=True)
    solved = chain_solve(everyone)
    return lax.dynamic_index_in_dim(solved, lax.axis_index("gx"), 0, keepdims=False)


def line_apply(grouped, matrices, couples):
    values = jnp.einsum("gic,cgm->igm", matrices, grouped, precision=PRECISE)
    group_count, column_count = (values.shape[1], values.shape[2])
    lower_couple = couples[0]
    upper_couple = couples[1]

    def spread(vector):
        return jnp.broadcast_to(vector[:, None], (group_count, column_count)).reshape(
            group_count * column_count
        )

    chain_local = jnp.stack(
        [
            values[0].reshape(-1),
            values[-1].reshape(-1),
            spread(lower_couple * matrices[:, 0, 0]),
            spread(lower_couple * matrices[:, -1, 0]),
            spread(upper_couple * matrices[:, 0, -1]),
            spread(upper_couple * matrices[:, -1, -1]),
        ]
    )
    solved = reduced_solve(chain_local)
    previous = solved[0].reshape(group_count, column_count)
    following = solved[1].reshape(group_count, column_count)
    first_column = jnp.transpose(matrices[:, :, 0])
    last_column = jnp.transpose(matrices[:, :, -1])
    return (
        values
        - (lower_couple[:, None] * previous)[None] * first_column[:, :, None]
        - (upper_couple[:, None] * following)[None] * last_column[:, :, None]
    )


def row_apply(rows, matrix, couple_pair):
    values = jnp.einsum("mc,ic->mi", rows, matrix, precision=PRECISE)
    lower_couple = couple_pair[0]
    upper_couple = couple_pair[1]
    line_count = values.shape[0]

    def spread(value):
        return jnp.broadcast_to(value, (line_count,))

    chain_local = jnp.stack(
        [
            values[:, 0],
            values[:, -1],
            spread(lower_couple * matrix[0, 0]),
            spread(lower_couple * matrix[-1, 0]),
            spread(upper_couple * matrix[0, -1]),
            spread(upper_couple * matrix[-1, -1]),
        ]
    )
    solved = reduced_solve(chain_local)
    return (
        values
        - (lower_couple * solved[0])[:, None] * matrix[:, 0][None, :]
        - (upper_couple * solved[1])[:, None] * matrix[:, -1][None, :]
    )


def local(
    source_field,
    permeability,
    layer_ids,
    inverse_fine,
    couple_fine,
    inverse_coarse,
    couple_coarse,
    owner_map,
):
    block_width, planes, depth_cells = source_field.shape
    layers = inverse_fine.shape[0]
    per_layer = depth_cells // layers
    order = jnp.argsort(layer_ids, stable=True)
    restore = jnp.argsort(order, stable=True)
    halo_permeability = with_halo(permeability, (("gx", 0), ("gy", 1)), 1)
    face_list = face_terms(padded_depth(halo_permeability))

    def residual_of(field_now):
        padded = with_halo(field_now, (("gx", 0), ("gy", 1)), 1)
        return source_field - apply_operator(padded_depth(padded), face_list)

    fine_couples = couple_fine[:, :, 0]
    solution = jnp.zeros_like(source_field)
    update = source_field
    for sweep_index in range(NSWEEP):
        if sweep_index > 0:
            update = residual_of(solution)
        ordered = jnp.take(update, order, axis=2).reshape(block_width, planes, layers, per_layer)
        change = line_apply(
            jnp.transpose(ordered, (0, 2, 1, 3)).reshape(block_width, layers, planes * per_layer),
            inverse_fine,
            fine_couples,
        )
        from_shaped = jnp.transpose(
            change.reshape(block_width, layers, planes, per_layer), (0, 2, 1, 3)
        )
        solution = solution + jnp.take(
            from_shaped.reshape(block_width, planes, depth_cells), restore, axis=2
        )
    residual = residual_of(solution)
    coarse = 0.5 * (residual[:, 0::2, :] + residual[:, 1::2, :])
    groups = lax.axis_size("gy")
    position = lax.axis_index("gy")
    chunk = depth_cells // groups
    aggregates = 8
    owners = owner_map[:, 0]
    coarse_rows = jnp.take(jnp.transpose(coarse[:, 0, :]), order, axis=0)
    pieces = lax.all_to_all(
        coarse_rows.reshape(groups, chunk, block_width), "gy", 0, 0, tiled=True
    )
    member = (owners[:, None] == jnp.arange(aggregates, dtype=jnp.int32)[None, :]).astype(
        jnp.float32
    )
    summed = jnp.einsum("jzx,jo->ozx", pieces, member, precision=PRECISE)
    own_layer = (position * chunk) // per_layer
    matrix = lax.dynamic_index_in_dim(inverse_coarse, own_layer, 0, keepdims=False)
    couples = lax.dynamic_index_in_dim(couple_coarse[:, :, 0], own_layer, 1, keepdims=False)
    smoothed = row_apply(summed.reshape(aggregates * chunk, block_width), matrix, couples)
    outgoing = jnp.take(smoothed.reshape(aggregates, chunk, block_width), owners, axis=0)
    returned = lax.all_to_all(outgoing, "gy", 0, 0, tiled=True)
    result = jnp.take(returned.reshape(depth_cells, block_width), restore, axis=0)
    return (solution, residual, jnp.transpose(result)[:, None, :])


def solution(mesh):
    in_specs = (
        P("gx", "gy", None),
        P("gx", "gy", None),
        P(),
        P(None, "gx", None),
        P(None, None, "gx"),
        P(None, "gx", None),
        P(None, None, "gx"),
        P(),
    )
    out_specs = (P("gx", "gy", None), P("gx", "gy", None), P("gx", "gy", None))
    return jax.shard_map(local, mesh=mesh, in_specs=in_specs, out_specs=out_specs, check_vma=False)
```

```python
import jax
import jax.numpy as jnp
from jax import lax
from jax.sharding import PartitionSpec as P

NSWEEP = 3


PRECISE = lax.Precision.HIGHEST
WEIGHTS = (0.5, 0.5, 0.15, 0.15, 0.05, 0.05)
STORAGE = 0.1


def with_halo(array, sides, width):
    for axis, dim in sides:
        peers, length = (lax.axis_size(axis), array.shape[dim])
        up = [(i, (i + 1) % peers) for i in range(peers - 1)]
        down = [(j, i) for i, j in up]
        last = lax.slice_in_dim(array, length - width, length, axis=dim)
        leading = lax.slice_in_dim(array, 0, width, axis=dim)
        before = lax.ppermute(last, axis, up)
        after = lax.ppermute(leading, axis, down)
        array = jnp.concatenate([before, array, after], axis=dim)
    return array


def neighbours(padded):
    return [
        padded[:-2, 1:-1, 1:-1],
        padded[2:, 1:-1, 1:-1],
        padded[1:-1, :-2, 1:-1],
        padded[1:-1, 2:, 1:-1],
        padded[1:-1, 1:-1, :-2],
        padded[1:-1, 1:-1, 2:],
    ]


def face_terms(padded):
    centre = padded[1:-1, 1:-1, 1:-1]
    return [
        weight * 2.0 * centre * beside / (centre + beside)
        for weight, beside in zip(WEIGHTS, neighbours(padded))
    ]


def apply_operator(padded, face_list):
    centre = padded[1:-1, 1:-1, 1:-1]
    result_sum = STORAGE * centre
    for face_term, beside in zip(face_list, neighbours(padded)):
        result_sum = result_sum + face_term * (centre - beside)
    return result_sum


def padded_depth(field_now):
    return jnp.pad(field_now, ((0, 0), (0, 0), (1, 1)))


def chain_solve(chain_rows):
    blocks_count = chain_rows.shape[0]
    carry_value = jnp.zeros_like(chain_rows[0, 0])
    carry_gain = jnp.zeros_like(chain_rows[0, 0])
    first_parts, first_links, last_parts, last_links = ([], [], [], [])
    for block_index in range(blocks_count):
        pivot_value = 1.0 - chain_rows[block_index, 2] * carry_gain
        first_part = (
            chain_rows[block_index, 0] - chain_rows[block_index, 2] * carry_value
        ) / pivot_value
        first_link = chain_rows[block_index, 4] / pivot_value
        carry_value = (
            chain_rows[block_index, 1]
            - chain_rows[block_index, 3] * carry_value
            + chain_rows[block_index, 3] * carry_gain * first_part
        )
        carry_gain = (
            chain_rows[block_index, 5] + chain_rows[block_index, 3] * carry_gain * first_link
        )
        first_parts.append(first_part)
        first_links.append(first_link)
        last_parts.append(carry_value)
        last_links.append(carry_gain)
    following = jnp.zeros_like(carry_value)
    last_values = [following] * blocks_count
    next_values = [following] * blocks_count
    for block_index in range(blocks_count - 1, -1, -1):
        next_values[block_index] = following
        last_values[block_index] = last_parts[block_index] - last_links[block_index] * following
        following = first_parts[block_index] - first_links[block_index] * following
    previous = [jnp.zeros_like(following)] + last_values[:-1]
    return jnp.stack(
        [
            jnp.stack([previous[block_index], next_values[block_index]])
            for block_index in range(blocks_count)
        ]
    )


def reduced_solve(chain_local):
    packed = chain_local[None]
    everyone = lax.all_gather(packed, "gx", axis=0, tiled=True)
    solved = chain_solve(everyone)
    return lax.dynamic_index_in_dim(solved, lax.axis_index("gx"), 0, keepdims=False)


def line_apply(grouped, matrices, couples):
    values = jnp.einsum("gic,cgm->igm", matrices, grouped, precision=PRECISE)
    group_count, column_count = (values.shape[1], values.shape[2])
    lower_couple = couples[0]
    upper_couple = couples[1]

    def spread(vector):
        return jnp.broadcast_to(vector[:, None], (group_count, column_count)).reshape(
            group_count * column_count
        )

    chain_local = jnp.stack(
        [
            values[0].reshape(-1),
            values[-1].reshape(-1),
            spread(lower_couple * matrices[:, 0, 0]),
            spread(lower_couple * matrices[:, -1, 0]),
            spread(upper_couple * matrices[:, 0, -1]),
            spread(upper_couple * matrices[:, -1, -1]),
        ]
    )
    solved = reduced_solve(chain_local)
    previous = solved[0].reshape(group_count, column_count)
    following = solved[1].reshape(group_count, column_count)
    first_column = jnp.transpose(matrices[:, :, 0])
    last_column = jnp.transpose(matrices[:, :, -1])
    return (
        values
        - (lower_couple[:, None] * previous)[None] * first_column[:, :, None]
        - (upper_couple[:, None] * following)[None] * last_column[:, :, None],
        previous,
        following,
    )


def row_apply(rows, matrix, couple_pair):
    values = jnp.einsum("mc,ic->mi", rows, matrix, precision=PRECISE)
    lower_couple = couple_pair[0]
    upper_couple = couple_pair[1]
    line_count = values.shape[0]

    def spread(value):
        return jnp.broadcast_to(value, (line_count,))

    chain_local = jnp.stack(
        [
            values[:, 0],
            values[:, -1],
            spread(lower_couple * matrix[0, 0]),
            spread(lower_couple * matrix[-1, 0]),
            spread(upper_couple * matrix[0, -1]),
            spread(upper_couple * matrix[-1, -1]),
        ]
    )
    solved = reduced_solve(chain_local)
    return (
        values
        - (lower_couple * solved[0])[:, None] * matrix[:, 0][None, :]
        - (upper_couple * solved[1])[:, None] * matrix[:, -1][None, :]
    )


def local(
    source_field,
    permeability,
    layer_ids,
    inverse_fine,
    couple_fine,
    inverse_coarse,
    couple_coarse,
    owner_map,
):
    block_width, planes, depth_cells = source_field.shape
    layers = inverse_fine.shape[0]
    per_layer = depth_cells // layers
    order = jnp.argsort(layer_ids, stable=True)
    restore = jnp.argsort(order, stable=True)
    halo_permeability = with_halo(permeability, (("gx", 0), ("gy", 1)), 1)
    face_list = face_terms(padded_depth(halo_permeability))
    rows = lax.axis_size("gy")
    up = [(i, i + 1) for i in range(rows - 1)]
    down = [(j, i) for i, j in up]

    def residual_of(field_now, left, right):
        lower = lax.ppermute(field_now[:, planes - 1 :, :], "gy", up)
        upper = lax.ppermute(field_now[:, :1, :], "gy", down)
        middle = jnp.concatenate([left, field_now, right], axis=0)
        rim = ((1, 1), (0, 0), (0, 0))
        padded = jnp.concatenate([jnp.pad(lower, rim), middle, jnp.pad(upper, rim)], axis=1)
        return source_field - apply_operator(padded_depth(padded), face_list)

    def unsorted(lines):
        shaped = jnp.transpose(lines.reshape(layers, planes, per_layer), (1, 0, 2))
        return jnp.take(shaped.reshape(planes, depth_cells), restore, axis=1)[None]

    fine_couples = couple_fine[:, :, 0]
    solution = jnp.zeros_like(source_field)
    left = jnp.zeros_like(source_field[:1])
    right = jnp.zeros_like(source_field[:1])
    update = source_field
    for sweep_index in range(NSWEEP):
        if sweep_index > 0:
            update = residual_of(solution, left, right)
        ordered = jnp.take(update, order, axis=2).reshape(block_width, planes, layers, per_layer)
        change, previous, following = line_apply(
            jnp.transpose(ordered, (0, 2, 1, 3)).reshape(block_width, layers, planes * per_layer),
            inverse_fine,
            fine_couples,
        )
        from_shaped = jnp.transpose(
            change.reshape(block_width, layers, planes, per_layer), (0, 2, 1, 3)
        )
        solution = solution + jnp.take(
            from_shaped.reshape(block_width, planes, depth_cells), restore, axis=2
        )
        left = left + unsorted(previous)
        right = right + unsorted(following)
    residual = residual_of(solution, left, right)
    coarse = 0.5 * (residual[:, 0::2, :] + residual[:, 1::2, :])
    groups = lax.axis_size("gy")
    position = lax.axis_index("gy")
    chunk = depth_cells // groups
    aggregates = 8
    owners = owner_map[:, 0]
    coarse_rows = jnp.take(jnp.transpose(coarse[:, 0, :]), order, axis=0)
    pieces = lax.all_to_all(
        coarse_rows.reshape(groups, chunk, block_width), "gy", 0, 0, tiled=True
    )
    member = (owners[:, None] == jnp.arange(aggregates, dtype=jnp.int32)[None, :]).astype(
        jnp.float32
    )
    summed = jnp.einsum("jzx,jo->ozx", pieces, member, precision=PRECISE)
    own_layer = (position * chunk) // per_layer
    matrix = lax.dynamic_index_in_dim(inverse_coarse, own_layer, 0, keepdims=False)
    couples = lax.dynamic_index_in_dim(couple_coarse[:, :, 0], own_layer, 1, keepdims=False)
    smoothed = row_apply(summed.reshape(aggregates * chunk, block_width), matrix, couples)
    outgoing = jnp.take(smoothed.reshape(aggregates, chunk, block_width), owners, axis=0)
    returned = lax.all_to_all(outgoing, "gy", 0, 0, tiled=True)
    result = jnp.take(returned.reshape(depth_cells, block_width), restore, axis=0)
    return (solution, residual, jnp.transpose(result)[:, None, :])


def solution(mesh):
    in_specs = (
        P("gx", "gy", None),
        P("gx", "gy", None),
        P(),
        P(None, "gx", None),
        P(None, None, "gx"),
        P(None, "gx", None),
        P(None, None, "gx"),
        P(),
    )
    out_specs = (P("gx", "gy", None), P("gx", "gy", None), P("gx", "gy", None))
    return jax.shard_map(local, mesh=mesh, in_specs=in_specs, out_specs=out_specs, check_vma=False)
```

```python
import jax
import jax.numpy as jnp
from jax import lax
from jax.sharding import PartitionSpec as P

NSWEEP = 3


PRECISE = lax.Precision.HIGHEST
WEIGHTS = (0.5, 0.5, 0.15, 0.15, 0.05, 0.05)
STORAGE = 0.1


def with_halo(array, sides, width):
    for axis, dim in sides:
        peers, length = (lax.axis_size(axis), array.shape[dim])
        up = [(i, (i + 1) % peers) for i in range(peers - 1)]
        down = [(j, i) for i, j in up]
        last = lax.slice_in_dim(array, length - width, length, axis=dim)
        leading = lax.slice_in_dim(array, 0, width, axis=dim)
        before = lax.ppermute(last, axis, up)
        after = lax.ppermute(leading, axis, down)
        array = jnp.concatenate([before, array, after], axis=dim)
    return array


def neighbours(padded):
    return [
        padded[:-2, 1:-1, 1:-1],
        padded[2:, 1:-1, 1:-1],
        padded[1:-1, :-2, 1:-1],
        padded[1:-1, 2:, 1:-1],
        padded[1:-1, 1:-1, :-2],
        padded[1:-1, 1:-1, 2:],
    ]


def face_terms(padded):
    centre = padded[1:-1, 1:-1, 1:-1]
    return [
        weight * 2.0 * centre * beside / (centre + beside)
        for weight, beside in zip(WEIGHTS, neighbours(padded))
    ]


def apply_operator(padded, face_list):
    centre = padded[1:-1, 1:-1, 1:-1]
    result_sum = STORAGE * centre
    for face_term, beside in zip(face_list, neighbours(padded)):
        result_sum = result_sum + face_term * (centre - beside)
    return result_sum


def padded_depth(field_now):
    return jnp.pad(field_now, ((0, 0), (0, 0), (1, 1)))


def chain_solve(chain_rows):
    blocks_count = chain_rows.shape[0]
    carry_value = jnp.zeros_like(chain_rows[0, 0])
    carry_gain = jnp.zeros_like(chain_rows[0, 0])
    first_parts, first_links, last_parts, last_links = ([], [], [], [])
    for block_index in range(blocks_count):
        pivot_value = 1.0 - chain_rows[block_index, 2] * carry_gain
        first_part = (
            chain_rows[block_index, 0] - chain_rows[block_index, 2] * carry_value
        ) / pivot_value
        first_link = chain_rows[block_index, 4] / pivot_value
        carry_value = (
            chain_rows[block_index, 1]
            - chain_rows[block_index, 3] * carry_value
            + chain_rows[block_index, 3] * carry_gain * first_part
        )
        carry_gain = (
            chain_rows[block_index, 5] + chain_rows[block_index, 3] * carry_gain * first_link
        )
        first_parts.append(first_part)
        first_links.append(first_link)
        last_parts.append(carry_value)
        last_links.append(carry_gain)
    following = jnp.zeros_like(carry_value)
    last_values = [following] * blocks_count
    next_values = [following] * blocks_count
    for block_index in range(blocks_count - 1, -1, -1):
        next_values[block_index] = following
        last_values[block_index] = last_parts[block_index] - last_links[block_index] * following
        following = first_parts[block_index] - first_links[block_index] * following
    previous = [jnp.zeros_like(following)] + last_values[:-1]
    return jnp.stack(
        [
            jnp.stack([previous[block_index], next_values[block_index]])
            for block_index in range(blocks_count)
        ]
    )


def reduced_solve(chain_local):
    peers = lax.axis_size("gx")
    packed = jnp.broadcast_to(chain_local[None], (peers,) + chain_local.shape)
    everyone = lax.all_to_all(packed, "gx", 0, 0, tiled=True)
    solved = chain_solve(everyone)
    return lax.dynamic_index_in_dim(solved, lax.axis_index("gx"), 0, keepdims=False)


def line_finish(values, matrices, couples):
    group_count, column_count = (values.shape[1], values.shape[2])
    lower_couple = couples[0]
    upper_couple = couples[1]

    def spread(vector):
        return jnp.broadcast_to(vector[:, None], (group_count, column_count)).reshape(
            group_count * column_count
        )

    chain_local = jnp.stack(
        [
            values[0].reshape(-1),
            values[-1].reshape(-1),
            spread(lower_couple * matrices[:, 0, 0]),
            spread(lower_couple * matrices[:, -1, 0]),
            spread(upper_couple * matrices[:, 0, -1]),
            spread(upper_couple * matrices[:, -1, -1]),
        ]
    )
    solved = reduced_solve(chain_local)
    previous = solved[0].reshape(group_count, column_count)
    following = solved[1].reshape(group_count, column_count)
    first_column = jnp.transpose(matrices[:, :, 0])
    last_column = jnp.transpose(matrices[:, :, -1])
    return (
        values
        - (lower_couple[:, None] * previous)[None] * first_column[:, :, None]
        - (upper_couple[:, None] * following)[None] * last_column[:, :, None],
        previous,
        following,
    )


def row_apply(rows, matrix, couple_pair):
    values = jnp.einsum("mc,ic->mi", rows, matrix, precision=PRECISE)
    lower_couple = couple_pair[0]
    upper_couple = couple_pair[1]
    line_count = values.shape[0]

    def spread(value):
        return jnp.broadcast_to(value, (line_count,))

    chain_local = jnp.stack(
        [
            values[:, 0],
            values[:, -1],
            spread(lower_couple * matrix[0, 0]),
            spread(lower_couple * matrix[-1, 0]),
            spread(upper_couple * matrix[0, -1]),
            spread(upper_couple * matrix[-1, -1]),
        ]
    )
    solved = reduced_solve(chain_local)
    return (
        values
        - (lower_couple * solved[0])[:, None] * matrix[:, 0][None, :]
        - (upper_couple * solved[1])[:, None] * matrix[:, -1][None, :]
    )


def local(
    source_field,
    permeability,
    layer_ids,
    inverse_fine,
    couple_fine,
    inverse_coarse,
    couple_coarse,
    owner_map,
):
    block_width, planes, depth_cells = source_field.shape
    layers = inverse_fine.shape[0]
    per_layer = depth_cells // layers
    order = jnp.argsort(layer_ids, stable=True)
    restore = jnp.argsort(order, stable=True)
    halo_permeability = with_halo(permeability, (("gx", 0), ("gy", 1)), 1)
    face_list = face_terms(padded_depth(halo_permeability))
    rows = lax.axis_size("gy")
    up = [(i, i + 1) for i in range(rows - 1)]
    down = [(j, i) for i, j in up]
    fine_couples = couple_fine[:, :, 0]
    lower_couple = fine_couples[0]
    upper_couple = fine_couples[1]
    first_column = jnp.transpose(inverse_fine[:, :, 0])
    last_column = jnp.transpose(inverse_fine[:, :, -1])
    top = (planes - 1) * per_layer

    def residual_of(field_now, left, right, lower, upper):
        middle = jnp.concatenate([left, field_now, right], axis=0)
        rim = ((1, 1), (0, 0), (0, 0))
        padded = jnp.concatenate([jnp.pad(lower, rim), middle, jnp.pad(upper, rim)], axis=1)
        return source_field - apply_operator(padded_depth(padded), face_list)

    def unsorted(lines):
        shaped = jnp.transpose(lines.reshape(layers, planes, per_layer), (1, 0, 2))
        return jnp.take(shaped.reshape(planes, depth_cells), restore, axis=1)[None]

    def rebuild(plane_values, ends):
        fixed = (
            plane_values
            - (lower_couple[:, None] * ends[0])[None] * first_column[:, :, None]
            - (upper_couple[:, None] * ends[1])[None] * last_column[:, :, None]
        )
        return jnp.take(fixed.reshape(block_width, depth_cells), restore, axis=1)[:, None, :]

    solution = jnp.zeros_like(source_field)
    left = jnp.zeros_like(source_field[:1])
    right = jnp.zeros_like(source_field[:1])
    lower = jnp.zeros_like(source_field[:, :1])
    upper = jnp.zeros_like(source_field[:, :1])
    update = source_field
    for sweep_index in range(NSWEEP):
        if sweep_index > 0:
            update = residual_of(solution, left, right, lower, upper)
        ordered = jnp.take(update, order, axis=2).reshape(block_width, planes, layers, per_layer)
        grouped = jnp.transpose(ordered, (0, 2, 1, 3)).reshape(
            block_width, layers, planes * per_layer
        )
        values = jnp.einsum("gic,cgm->igm", inverse_fine, grouped, precision=PRECISE)
        lower_values = lax.ppermute(values[:, :, top:], "gy", up)
        upper_values = lax.ppermute(values[:, :, :per_layer], "gy", down)
        change, previous, following = line_finish(values, inverse_fine, fine_couples)
        ends = jnp.stack([previous, following])
        lower_ends = lax.ppermute(ends[:, :, top:], "gy", up)
        upper_ends = lax.ppermute(ends[:, :, :per_layer], "gy", down)
        lower = lower + rebuild(lower_values, lower_ends)
        upper = upper + rebuild(upper_values, upper_ends)
        from_shaped = jnp.transpose(
            change.reshape(block_width, layers, planes, per_layer), (0, 2, 1, 3)
        )
        solution = solution + jnp.take(
            from_shaped.reshape(block_width, planes, depth_cells), restore, axis=2
        )
        left = left + unsorted(previous)
        right = right + unsorted(following)
    residual = residual_of(solution, left, right, lower, upper)
    coarse = 0.5 * (residual[:, 0::2, :] + residual[:, 1::2, :])
    groups = lax.axis_size("gy")
    position = lax.axis_index("gy")
    chunk = depth_cells // groups
    aggregates = 8
    owners = owner_map[:, 0]
    coarse_rows = jnp.take(jnp.transpose(coarse[:, 0, :]), order, axis=0)
    pieces = lax.all_to_all(
        coarse_rows.reshape(groups, chunk, block_width), "gy", 0, 0, tiled=True
    )
    member = (owners[:, None] == jnp.arange(aggregates, dtype=jnp.int32)[None, :]).astype(
        jnp.float32
    )
    summed = jnp.einsum("jzx,jo->ozx", pieces, member, precision=PRECISE)
    own_layer = (position * chunk) // per_layer
    matrix = lax.dynamic_index_in_dim(inverse_coarse, own_layer, 0, keepdims=False)
    couples = lax.dynamic_index_in_dim(couple_coarse[:, :, 0], own_layer, 1, keepdims=False)
    smoothed = row_apply(summed.reshape(aggregates * chunk, block_width), matrix, couples)
    outgoing = jnp.take(smoothed.reshape(aggregates, chunk, block_width), owners, axis=0)
    returned = lax.all_to_all(outgoing, "gy", 0, 0, tiled=True)
    result = jnp.take(returned.reshape(depth_cells, block_width), restore, axis=0)
    return (solution, residual, jnp.transpose(result)[:, None, :])


def solution(mesh):
    in_specs = (
        P("gx", "gy", None),
        P("gx", "gy", None),
        P(),
        P(None, "gx", None),
        P(None, None, "gx"),
        P(None, "gx", None),
        P(None, None, "gx"),
        P(),
    )
    out_specs = (P("gx", "gy", None), P("gx", "gy", None), P("gx", "gy", None))
    return jax.shard_map(local, mesh=mesh, in_specs=in_specs, out_specs=out_specs, check_vma=False)
```

```python
import jax
import jax.numpy as jnp
from jax import lax
from jax.sharding import PartitionSpec as P

NSWEEP = 3


PRECISE = lax.Precision.HIGHEST
WEIGHTS = (0.5, 0.5, 0.15, 0.15, 0.05, 0.05)
STORAGE = 0.1


def with_halo(array, sides, width):
    for axis, dim in sides:
        peers, length = (lax.axis_size(axis), array.shape[dim])
        up = [(i, (i + 1) % peers) for i in range(peers - 1)]
        down = [(j, i) for i, j in up]
        last = lax.slice_in_dim(array, length - width, length, axis=dim)
        leading = lax.slice_in_dim(array, 0, width, axis=dim)
        before = lax.ppermute(last, axis, up)
        after = lax.ppermute(leading, axis, down)
        array = jnp.concatenate([before, array, after], axis=dim)
    return array


def neighbours(padded):
    return [
        padded[:-2, 1:-1, 1:-1],
        padded[2:, 1:-1, 1:-1],
        padded[1:-1, :-2, 1:-1],
        padded[1:-1, 2:, 1:-1],
        padded[1:-1, 1:-1, :-2],
        padded[1:-1, 1:-1, 2:],
    ]


def face_terms(padded):
    centre = padded[1:-1, 1:-1, 1:-1]
    return [
        weight * 2.0 * centre * beside / (centre + beside)
        for weight, beside in zip(WEIGHTS, neighbours(padded))
    ]


def apply_operator(padded, face_list):
    centre = padded[1:-1, 1:-1, 1:-1]
    result_sum = STORAGE * centre
    for face_term, beside in zip(face_list, neighbours(padded)):
        result_sum = result_sum + face_term * (centre - beside)
    return result_sum


def padded_depth(field_now):
    return jnp.pad(field_now, ((0, 0), (0, 0), (1, 1)))


def chain_solve(chain_rows):
    blocks_count = chain_rows.shape[0]
    carry_value = jnp.zeros_like(chain_rows[0, 0])
    carry_gain = jnp.zeros_like(chain_rows[0, 0])
    first_parts, first_links, last_parts, last_links = ([], [], [], [])
    for block_index in range(blocks_count):
        pivot_value = 1.0 - chain_rows[block_index, 2] * carry_gain
        first_part = (
            chain_rows[block_index, 0] - chain_rows[block_index, 2] * carry_value
        ) / pivot_value
        first_link = chain_rows[block_index, 4] / pivot_value
        carry_value = (
            chain_rows[block_index, 1]
            - chain_rows[block_index, 3] * carry_value
            + chain_rows[block_index, 3] * carry_gain * first_part
        )
        carry_gain = (
            chain_rows[block_index, 5] + chain_rows[block_index, 3] * carry_gain * first_link
        )
        first_parts.append(first_part)
        first_links.append(first_link)
        last_parts.append(carry_value)
        last_links.append(carry_gain)
    following = jnp.zeros_like(carry_value)
    last_values = [following] * blocks_count
    next_values = [following] * blocks_count
    for block_index in range(blocks_count - 1, -1, -1):
        next_values[block_index] = following
        last_values[block_index] = last_parts[block_index] - last_links[block_index] * following
        following = first_parts[block_index] - first_links[block_index] * following
    previous = [jnp.zeros_like(following)] + last_values[:-1]
    return jnp.stack(
        [
            jnp.stack([previous[block_index], next_values[block_index]])
            for block_index in range(blocks_count)
        ]
    )


def reduced_solve(chain_local):
    peers = lax.axis_size("gx")
    packed = jnp.broadcast_to(chain_local[None], (peers,) + chain_local.shape)
    everyone = lax.all_to_all(packed, "gx", 0, 0, tiled=True)
    solved = chain_solve(everyone)
    return lax.dynamic_index_in_dim(solved, lax.axis_index("gx"), 0, keepdims=False)


def line_apply(grouped, matrices, couples):
    values = jnp.einsum("gic,cgm->igm", matrices, grouped, precision=PRECISE)
    group_count, column_count = (values.shape[1], values.shape[2])
    lower_couple = couples[0]
    upper_couple = couples[1]

    def spread(vector):
        return jnp.broadcast_to(vector[:, None], (group_count, column_count)).reshape(
            group_count * column_count
        )

    chain_local = jnp.stack(
        [
            values[0].reshape(-1),
            values[-1].reshape(-1),
            spread(lower_couple * matrices[:, 0, 0]),
            spread(lower_couple * matrices[:, -1, 0]),
            spread(upper_couple * matrices[:, 0, -1]),
            spread(upper_couple * matrices[:, -1, -1]),
        ]
    )
    solved = reduced_solve(chain_local)
    previous = solved[0].reshape(group_count, column_count)
    following = solved[1].reshape(group_count, column_count)
    first_column = jnp.transpose(matrices[:, :, 0])
    last_column = jnp.transpose(matrices[:, :, -1])
    return (
        values
        - (lower_couple[:, None] * previous)[None] * first_column[:, :, None]
        - (upper_couple[:, None] * following)[None] * last_column[:, :, None],
        previous,
        following,
    )


def row_apply(rows, matrix, couple_pair):
    values = jnp.einsum("mc,ic->mi", rows, matrix, precision=PRECISE)
    lower_couple = couple_pair[0]
    upper_couple = couple_pair[1]
    line_count = values.shape[0]

    def spread(value):
        return jnp.broadcast_to(value, (line_count,))

    chain_local = jnp.stack(
        [
            values[:, 0],
            values[:, -1],
            spread(lower_couple * matrix[0, 0]),
            spread(lower_couple * matrix[-1, 0]),
            spread(upper_couple * matrix[0, -1]),
            spread(upper_couple * matrix[-1, -1]),
        ]
    )
    solved = reduced_solve(chain_local)
    return (
        values
        - (lower_couple * solved[0])[:, None] * matrix[:, 0][None, :]
        - (upper_couple * solved[1])[:, None] * matrix[:, -1][None, :]
    )


def local(
    source_field,
    permeability,
    layer_ids,
    inverse_fine,
    couple_fine,
    inverse_coarse,
    couple_coarse,
    owner_map,
):
    block_width, planes, depth_cells = source_field.shape
    layers = inverse_fine.shape[0]
    per_layer = depth_cells // layers
    order = jnp.argsort(layer_ids, stable=True)
    restore = jnp.argsort(order, stable=True)
    halo_permeability = with_halo(permeability, (("gx", 0), ("gy", 1)), 1)
    face_list = face_terms(padded_depth(halo_permeability))
    rows = lax.axis_size("gy")
    up = [(i, i + 1) for i in range(rows - 1)]
    down = [(j, i) for i, j in up]

    def residual_of(field_now, left, right):
        lower = lax.ppermute(field_now[:, planes - 1 :, :], "gy", up)
        upper = lax.ppermute(field_now[:, :1, :], "gy", down)
        middle = jnp.concatenate([left, field_now, right], axis=0)
        rim = ((1, 1), (0, 0), (0, 0))
        padded = jnp.concatenate([jnp.pad(lower, rim), middle, jnp.pad(upper, rim)], axis=1)
        return source_field - apply_operator(padded_depth(padded), face_list)

    def unsorted(lines):
        shaped = jnp.transpose(lines.reshape(layers, planes, per_layer), (1, 0, 2))
        return jnp.take(shaped.reshape(planes, depth_cells), restore, axis=1)[None]

    fine_couples = couple_fine[:, :, 0]
    solution = jnp.zeros_like(source_field)
    left = jnp.zeros_like(source_field[:1])
    right = jnp.zeros_like(source_field[:1])
    update = source_field
    for sweep_index in range(NSWEEP):
        if sweep_index > 0:
            update = residual_of(solution, left, right)
        ordered = jnp.take(update, order, axis=2).reshape(block_width, planes, layers, per_layer)
        change, previous, following = line_apply(
            jnp.transpose(ordered, (0, 2, 1, 3)).reshape(block_width, layers, planes * per_layer),
            inverse_fine,
            fine_couples,
        )
        from_shaped = jnp.transpose(
            change.reshape(block_width, layers, planes, per_layer), (0, 2, 1, 3)
        )
        solution = solution + jnp.take(
            from_shaped.reshape(block_width, planes, depth_cells), restore, axis=2
        )
        left = left + unsorted(previous)
        right = right + unsorted(following)
    residual = residual_of(solution, left, right)
    coarse = 0.5 * (residual[:, 0::2, :] + residual[:, 1::2, :])
    groups = lax.axis_size("gy")
    position = lax.axis_index("gy")
    chunk = depth_cells // groups
    aggregates = 8
    owners = owner_map[:, 0]
    coarse_rows = jnp.take(jnp.transpose(coarse[:, 0, :]), order, axis=0)
    pieces = lax.all_to_all(
        coarse_rows.reshape(groups, chunk, block_width), "gy", 0, 0, tiled=True
    )
    member = (owners[:, None] == jnp.arange(aggregates, dtype=jnp.int32)[None, :]).astype(
        jnp.float32
    )
    summed = jnp.einsum("jzx,jo->ozx", pieces, member, precision=PRECISE)
    own_layer = (position * chunk) // per_layer
    matrix = lax.dynamic_index_in_dim(inverse_coarse, own_layer, 0, keepdims=False)
    couples = lax.dynamic_index_in_dim(couple_coarse[:, :, 0], own_layer, 1, keepdims=False)
    smoothed = row_apply(summed.reshape(aggregates * chunk, block_width), matrix, couples)
    outgoing = jnp.take(smoothed.reshape(aggregates, chunk, block_width), owners, axis=0)
    returned = lax.all_to_all(outgoing, "gy", 0, 0, tiled=True)
    result = jnp.take(returned.reshape(depth_cells, block_width), restore, axis=0)
    return (solution, residual, jnp.transpose(result)[:, None, :])


def solution(mesh):
    in_specs = (
        P("gx", "gy", None),
        P("gx", "gy", None),
        P(),
        P(None, "gx", None),
        P(None, None, "gx"),
        P(None, "gx", None),
        P(None, None, "gx"),
        P(),
    )
    out_specs = (P("gx", "gy", None), P("gx", "gy", None), P("gx", "gy", None))
    return jax.shard_map(local, mesh=mesh, in_specs=in_specs, out_specs=out_specs, check_vma=False)
```

```python
import jax
import jax.numpy as jnp
from jax import lax
from jax.sharding import PartitionSpec as P

NSWEEP = 3


PRECISE = lax.Precision.HIGHEST
WEIGHTS = (0.5, 0.5, 0.15, 0.15, 0.05, 0.05)
STORAGE = 0.1


def with_halo(array, sides, width):
    for axis, dim in sides:
        peers, length = (lax.axis_size(axis), array.shape[dim])
        up = [(i, (i + 1) % peers) for i in range(peers - 1)]
        down = [(j, i) for i, j in up]
        last = lax.slice_in_dim(array, length - width, length, axis=dim)
        leading = lax.slice_in_dim(array, 0, width, axis=dim)
        before = lax.ppermute(last, axis, up)
        after = lax.ppermute(leading, axis, down)
        array = jnp.concatenate([before, array, after], axis=dim)
    return array


def neighbours(padded):
    return [
        padded[1:-1, 1:-1, :-2],
        padded[1:-1, 1:-1, 2:],
        padded[:-2, 1:-1, 1:-1],
        padded[2:, 1:-1, 1:-1],
        padded[1:-1, :-2, 1:-1],
        padded[1:-1, 2:, 1:-1],
    ]


def face_terms(padded):
    centre = padded[1:-1, 1:-1, 1:-1]
    return [
        weight * 2.0 * centre * beside / (centre + beside)
        for weight, beside in zip(WEIGHTS, neighbours(padded))
    ]


def apply_operator(padded, face_list):
    centre = padded[1:-1, 1:-1, 1:-1]
    result_sum = STORAGE * centre
    for face_term, beside in zip(face_list, neighbours(padded)):
        result_sum = result_sum + face_term * (centre - beside)
    return result_sum


def padded_depth(field_now):
    return jnp.pad(field_now, ((0, 0), (1, 1), (0, 0)))


def chain_solve(chain_rows):
    blocks_count = chain_rows.shape[0]
    carry_value = jnp.zeros_like(chain_rows[0, 0])
    carry_gain = jnp.zeros_like(chain_rows[0, 0])
    first_parts, first_links, last_parts, last_links = ([], [], [], [])
    for block_index in range(blocks_count):
        pivot_value = 1.0 - chain_rows[block_index, 2] * carry_gain
        first_part = (
            chain_rows[block_index, 0] - chain_rows[block_index, 2] * carry_value
        ) / pivot_value
        first_link = chain_rows[block_index, 4] / pivot_value
        carry_value = (
            chain_rows[block_index, 1]
            - chain_rows[block_index, 3] * carry_value
            + chain_rows[block_index, 3] * carry_gain * first_part
        )
        carry_gain = (
            chain_rows[block_index, 5] + chain_rows[block_index, 3] * carry_gain * first_link
        )
        first_parts.append(first_part)
        first_links.append(first_link)
        last_parts.append(carry_value)
        last_links.append(carry_gain)
    following = jnp.zeros_like(carry_value)
    last_values = [following] * blocks_count
    next_values = [following] * blocks_count
    for block_index in range(blocks_count - 1, -1, -1):
        next_values[block_index] = following
        last_values[block_index] = last_parts[block_index] - last_links[block_index] * following
        following = first_parts[block_index] - first_links[block_index] * following
    previous = [jnp.zeros_like(following)] + last_values[:-1]
    return jnp.stack(
        [
            jnp.stack([previous[block_index], next_values[block_index]])
            for block_index in range(blocks_count)
        ]
    )


def reduced_solve(chain_local):
    peers = lax.axis_size("gx")
    packed = jnp.broadcast_to(chain_local[None], (peers,) + chain_local.shape)
    everyone = lax.all_to_all(packed, "gx", 0, 0, tiled=True)
    solved = chain_solve(everyone)
    return lax.dynamic_index_in_dim(solved, lax.axis_index("gx"), 0, keepdims=False)


def row_apply(rows, matrix, couple_pair):
    values = jnp.einsum("mc,ic->mi", rows, matrix, precision=PRECISE)
    lower_couple = couple_pair[0]
    upper_couple = couple_pair[1]
    line_count = values.shape[0]

    def spread(value):
        return jnp.broadcast_to(value, (line_count,))

    chain_local = jnp.stack(
        [
            values[:, 0],
            values[:, -1],
            spread(lower_couple * matrix[0, 0]),
            spread(lower_couple * matrix[-1, 0]),
            spread(upper_couple * matrix[0, -1]),
            spread(upper_couple * matrix[-1, -1]),
        ]
    )
    solved = reduced_solve(chain_local)
    return (
        values
        - (lower_couple * solved[0])[:, None] * matrix[:, 0][None, :]
        - (upper_couple * solved[1])[:, None] * matrix[:, -1][None, :]
    )


def sorted_positions(layer_ids, layers, per_layer):
    depth_cells = layer_ids.shape[0]
    kinds = jnp.arange(layers, dtype=jnp.int32)
    onehot = (layer_ids[:, None] == kinds[None, :]).astype(jnp.int32)
    before = jnp.cumsum(onehot, axis=0) - onehot
    restore = jnp.sum(onehot * (before + kinds[None, :] * per_layer), axis=1)
    cells = jnp.arange(depth_cells, dtype=jnp.int32)
    order = jnp.sum(jnp.where(restore[None, :] == cells[:, None], cells[None, :], 0), axis=1)
    return order, restore


def local(
    source_field,
    permeability,
    layer_ids,
    inverse_fine,
    couple_fine,
    inverse_coarse,
    couple_coarse,
    owner_map,
):
    block_width, planes, depth_cells = source_field.shape
    layers = inverse_fine.shape[0]
    per_layer = depth_cells // layers
    order, restore = sorted_positions(layer_ids, layers, per_layer)
    source_t = jnp.transpose(source_field, (1, 2, 0))
    halo_permeability = with_halo(
        jnp.transpose(permeability, (1, 2, 0)), (("gx", 2), ("gy", 0)), 1
    )
    face_list = face_terms(padded_depth(halo_permeability))
    rows = lax.axis_size("gy")
    up = [(i, i + 1) for i in range(rows - 1)]
    down = [(j, i) for i, j in up]
    lower_couple = couple_fine[0, :, 0]
    upper_couple = couple_fine[1, :, 0]
    first_column = inverse_fine[:, :, 0][None, :, None, :]
    last_column = inverse_fine[:, :, -1][None, :, None, :]
    shaped = (planes, layers, per_layer)

    def spread(vector):
        return jnp.broadcast_to(vector[None, :, None], shaped).reshape(-1)

    constants = [
        spread(lower_couple * inverse_fine[:, 0, 0]),
        spread(lower_couple * inverse_fine[:, -1, 0]),
        spread(upper_couple * inverse_fine[:, 0, -1]),
        spread(upper_couple * inverse_fine[:, -1, -1]),
    ]

    def residual_of(field_now, left, right):
        lower = lax.ppermute(field_now[planes - 1 :], "gy", up)
        upper = lax.ppermute(field_now[:1], "gy", down)
        middle = jnp.concatenate([left, field_now, right], axis=2)
        rim = ((0, 0), (0, 0), (1, 1))
        padded = jnp.concatenate([jnp.pad(lower, rim), middle, jnp.pad(upper, rim)], axis=0)
        return source_t - apply_operator(padded_depth(padded), face_list)

    def natural(lines):
        return jnp.take(lines.reshape(planes, depth_cells, -1), restore, axis=1)

    solution = jnp.zeros_like(source_t)
    left = jnp.zeros_like(source_t[:, :, :1])
    right = jnp.zeros_like(source_t[:, :, :1])
    update = source_t
    for sweep_index in range(NSWEEP):
        if sweep_index > 0:
            update = residual_of(solution, left, right)
        ordered = jnp.take(update, order, axis=1).reshape(planes, layers, per_layer, block_width)
        values = jnp.einsum("ygkc,gic->ygki", ordered, inverse_fine, precision=PRECISE)
        chain_local = jnp.stack(
            [values[..., 0].reshape(-1), values[..., -1].reshape(-1)] + constants
        )
        solved = reduced_solve(chain_local)
        previous = solved[0].reshape(shaped)
        following = solved[1].reshape(shaped)
        change = (
            values
            - (lower_couple[None, :, None] * previous)[..., None] * first_column
            - (upper_couple[None, :, None] * following)[..., None] * last_column
        )
        solution = solution + natural(change)
        left = left + natural(previous)
        right = right + natural(following)
    residual_t = residual_of(solution, left, right)
    coarse = 0.5 * (residual_t[0::2] + residual_t[1::2])
    groups = lax.axis_size("gy")
    position = lax.axis_index("gy")
    chunk = depth_cells // groups
    aggregates = 8
    owners = owner_map[:, 0]
    coarse_rows = jnp.take(coarse[0], order, axis=0)
    pieces = lax.all_to_all(
        coarse_rows.reshape(groups, chunk, block_width), "gy", 0, 0, tiled=True
    )
    member = (owners[:, None] == jnp.arange(aggregates, dtype=jnp.int32)[None, :]).astype(
        jnp.float32
    )
    summed = jnp.einsum("jzx,jo->ozx", pieces, member, precision=PRECISE)
    own_layer = (position * chunk) // per_layer
    matrix = lax.dynamic_index_in_dim(inverse_coarse, own_layer, 0, keepdims=False)
    couples = lax.dynamic_index_in_dim(couple_coarse[:, :, 0], own_layer, 1, keepdims=False)
    smoothed = row_apply(summed.reshape(aggregates * chunk, block_width), matrix, couples)
    outgoing = jnp.take(smoothed.reshape(aggregates, chunk, block_width), owners, axis=0)
    returned = lax.all_to_all(outgoing, "gy", 0, 0, tiled=True)
    result = jnp.take(returned.reshape(depth_cells, block_width), restore, axis=0)
    return (
        jnp.transpose(solution, (2, 0, 1)),
        jnp.transpose(residual_t, (2, 0, 1)),
        jnp.transpose(result)[:, None, :],
    )


def solution(mesh):
    in_specs = (
        P("gx", "gy", None),
        P("gx", "gy", None),
        P(),
        P(None, "gx", None),
        P(None, None, "gx"),
        P(None, "gx", None),
        P(None, None, "gx"),
        P(),
    )
    out_specs = (P("gx", "gy", None), P("gx", "gy", None), P("gx", "gy", None))
    return jax.shard_map(local, mesh=mesh, in_specs=in_specs, out_specs=out_specs, check_vma=False)
```

```python
import jax
import jax.numpy as jnp
from jax import lax
from jax.sharding import PartitionSpec as P

NSWEEP = 3


PRECISE = lax.Precision.HIGHEST
WEIGHTS = (0.5, 0.5, 0.15, 0.15, 0.05, 0.05)
STORAGE = 0.1


def with_halo(array, sides, width):
    for axis, dim in sides:
        peers, length = (lax.axis_size(axis), array.shape[dim])
        up = [(i, (i + 1) % peers) for i in range(peers - 1)]
        down = [(j, i) for i, j in up]
        last = lax.slice_in_dim(array, length - width, length, axis=dim)
        leading = lax.slice_in_dim(array, 0, width, axis=dim)
        before = lax.ppermute(last, axis, up)
        after = lax.ppermute(leading, axis, down)
        array = jnp.concatenate([before, array, after], axis=dim)
    return array


def neighbours(padded):
    return [
        padded[:-2, 1:-1, 1:-1],
        padded[2:, 1:-1, 1:-1],
        padded[1:-1, :-2, 1:-1],
        padded[1:-1, 2:, 1:-1],
        padded[1:-1, 1:-1, :-2],
        padded[1:-1, 1:-1, 2:],
    ]


def face_terms(padded):
    centre = padded[1:-1, 1:-1, 1:-1]
    return [
        weight * 2.0 * centre * beside / (centre + beside)
        for weight, beside in zip(WEIGHTS, neighbours(padded))
    ]


def apply_operator(padded, face_list):
    centre = padded[1:-1, 1:-1, 1:-1]
    result_sum = STORAGE * centre
    for face_term, beside in zip(face_list, neighbours(padded)):
        result_sum = result_sum + face_term * (centre - beside)
    return result_sum


def padded_depth(field_now):
    return jnp.pad(field_now, ((0, 0), (0, 0), (1, 1)))


def chain_solve(chain_rows):
    blocks_count = chain_rows.shape[0]
    carry_value = jnp.zeros_like(chain_rows[0, 0])
    carry_gain = jnp.zeros_like(chain_rows[0, 0])
    first_parts, first_links, last_parts, last_links = ([], [], [], [])
    for block_index in range(blocks_count):
        pivot_value = 1.0 - chain_rows[block_index, 2] * carry_gain
        first_part = (
            chain_rows[block_index, 0] - chain_rows[block_index, 2] * carry_value
        ) / pivot_value
        first_link = chain_rows[block_index, 4] / pivot_value
        carry_value = (
            chain_rows[block_index, 1]
            - chain_rows[block_index, 3] * carry_value
            + chain_rows[block_index, 3] * carry_gain * first_part
        )
        carry_gain = (
            chain_rows[block_index, 5] + chain_rows[block_index, 3] * carry_gain * first_link
        )
        first_parts.append(first_part)
        first_links.append(first_link)
        last_parts.append(carry_value)
        last_links.append(carry_gain)
    following = jnp.zeros_like(carry_value)
    last_values = [following] * blocks_count
    next_values = [following] * blocks_count
    for block_index in range(blocks_count - 1, -1, -1):
        next_values[block_index] = following
        last_values[block_index] = last_parts[block_index] - last_links[block_index] * following
        following = first_parts[block_index] - first_links[block_index] * following
    previous = [jnp.zeros_like(following)] + last_values[:-1]
    return jnp.stack(
        [
            jnp.stack([previous[block_index], next_values[block_index]])
            for block_index in range(blocks_count)
        ]
    )


def reduced_solve(chain_local):
    peers = lax.axis_size("gx")
    packed = jnp.broadcast_to(chain_local[None], (peers,) + chain_local.shape)
    everyone = lax.all_to_all(packed, "gx", 0, 0, tiled=True)
    solved = chain_solve(everyone)
    return lax.dynamic_index_in_dim(solved, lax.axis_index("gx"), 0, keepdims=False)


def line_apply(grouped, matrices, couples):
    values = jnp.einsum("gic,cgm->igm", matrices, grouped, precision=PRECISE)
    group_count, column_count = (values.shape[1], values.shape[2])
    lower_couple = couples[0]
    upper_couple = couples[1]

    def spread(vector):
        return jnp.broadcast_to(vector[:, None], (group_count, column_count)).reshape(
            group_count * column_count
        )

    chain_local = jnp.stack(
        [
            values[0].reshape(-1),
            values[-1].reshape(-1),
            spread(lower_couple * matrices[:, 0, 0]),
            spread(lower_couple * matrices[:, -1, 0]),
            spread(upper_couple * matrices[:, 0, -1]),
            spread(upper_couple * matrices[:, -1, -1]),
        ]
    )
    solved = reduced_solve(chain_local)
    previous = solved[0].reshape(group_count, column_count)
    following = solved[1].reshape(group_count, column_count)
    first_column = jnp.transpose(matrices[:, :, 0])
    last_column = jnp.transpose(matrices[:, :, -1])
    return (
        values
        - (lower_couple[:, None] * previous)[None] * first_column[:, :, None]
        - (upper_couple[:, None] * following)[None] * last_column[:, :, None],
        previous,
        following,
    )


def row_apply(rows, matrix, couple_pair):
    values = jnp.einsum("mc,ic->mi", rows, matrix, precision=PRECISE)
    lower_couple = couple_pair[0]
    upper_couple = couple_pair[1]
    line_count = values.shape[0]

    def spread(value):
        return jnp.broadcast_to(value, (line_count,))

    chain_local = jnp.stack(
        [
            values[:, 0],
            values[:, -1],
            spread(lower_couple * matrix[0, 0]),
            spread(lower_couple * matrix[-1, 0]),
            spread(upper_couple * matrix[0, -1]),
            spread(upper_couple * matrix[-1, -1]),
        ]
    )
    solved = reduced_solve(chain_local)
    return (
        values
        - (lower_couple * solved[0])[:, None] * matrix[:, 0][None, :]
        - (upper_couple * solved[1])[:, None] * matrix[:, -1][None, :]
    )


def sorted_positions(layer_ids, layers, per_layer):
    depth_cells = layer_ids.shape[0]
    kinds = jnp.arange(layers, dtype=jnp.int32)
    onehot = (layer_ids[:, None] == kinds[None, :]).astype(jnp.int32)
    before = jnp.cumsum(onehot, axis=0) - onehot
    restore = jnp.sum(onehot * (before + kinds[None, :] * per_layer), axis=1)
    cells = jnp.arange(depth_cells, dtype=jnp.int32)
    order = jnp.sum(jnp.where(restore[None, :] == cells[:, None], cells[None, :], 0), axis=1)
    return order, restore


def local(
    source_field,
    permeability,
    layer_ids,
    inverse_fine,
    couple_fine,
    inverse_coarse,
    couple_coarse,
    owner_map,
):
    block_width, planes, depth_cells = source_field.shape
    layers = inverse_fine.shape[0]
    per_layer = depth_cells // layers
    order, restore = sorted_positions(layer_ids, layers, per_layer)
    halo_permeability = with_halo(permeability, (("gx", 0), ("gy", 1)), 1)
    face_list = face_terms(padded_depth(halo_permeability))
    rows = lax.axis_size("gy")
    up = [(i, i + 1) for i in range(rows - 1)]
    down = [(j, i) for i, j in up]

    def residual_of(field_now, left, right):
        lower = lax.ppermute(field_now[:, planes - 1 :, :], "gy", up)
        upper = lax.ppermute(field_now[:, :1, :], "gy", down)
        middle = jnp.concatenate([left, field_now, right], axis=0)
        padded = jnp.pad(middle, ((0, 0), (1, 1), (0, 0)))
        partial = source_field - apply_operator(padded_depth(padded), face_list)
        return (
            partial.at[:, :1, :]
            .add(face_list[2][:, :1, :] * lower)
            .at[:, planes - 1 :, :]
            .add(face_list[3][:, planes - 1 :, :] * upper)
        )

    def unsorted(lines):
        shaped = jnp.transpose(lines.reshape(layers, planes, per_layer), (1, 0, 2))
        return jnp.take(shaped.reshape(planes, depth_cells), restore, axis=1)[None]

    fine_couples = couple_fine[:, :, 0]
    solution = jnp.zeros_like(source_field)
    left = jnp.zeros_like(source_field[:1])
    right = jnp.zeros_like(source_field[:1])
    update = source_field
    for sweep_index in range(NSWEEP):
        if sweep_index > 0:
            update = residual_of(solution, left, right)
        ordered = jnp.take(update, order, axis=2).reshape(block_width, planes, layers, per_layer)
        change, previous, following = line_apply(
            jnp.transpose(ordered, (0, 2, 1, 3)).reshape(block_width, layers, planes * per_layer),
            inverse_fine,
            fine_couples,
        )
        from_shaped = jnp.transpose(
            change.reshape(block_width, layers, planes, per_layer), (0, 2, 1, 3)
        )
        solution = solution + jnp.take(
            from_shaped.reshape(block_width, planes, depth_cells), restore, axis=2
        )
        left = left + unsorted(previous)
        right = right + unsorted(following)
    residual = residual_of(solution, left, right)
    coarse = 0.5 * (residual[:, 0::2, :] + residual[:, 1::2, :])
    groups = lax.axis_size("gy")
    position = lax.axis_index("gy")
    chunk = depth_cells // groups
    aggregates = 8
    owners = owner_map[:, 0]
    coarse_rows = jnp.take(jnp.transpose(coarse[:, 0, :]), order, axis=0)
    pieces = lax.all_to_all(
        coarse_rows.reshape(groups, chunk, block_width), "gy", 0, 0, tiled=True
    )
    member = (owners[:, None] == jnp.arange(aggregates, dtype=jnp.int32)[None, :]).astype(
        jnp.float32
    )
    summed = jnp.einsum("jzx,jo->ozx", pieces, member, precision=PRECISE)
    own_layer = (position * chunk) // per_layer
    matrix = lax.dynamic_index_in_dim(inverse_coarse, own_layer, 0, keepdims=False)
    couples = lax.dynamic_index_in_dim(couple_coarse[:, :, 0], own_layer, 1, keepdims=False)
    smoothed = row_apply(summed.reshape(aggregates * chunk, block_width), matrix, couples)
    outgoing = jnp.take(smoothed.reshape(aggregates, chunk, block_width), owners, axis=0)
    returned = lax.all_to_all(outgoing, "gy", 0, 0, tiled=True)
    result = jnp.take(returned.reshape(depth_cells, block_width), restore, axis=0)
    return (solution, residual, jnp.transpose(result)[:, None, :])


def solution(mesh):
    in_specs = (
        P("gx", "gy", None),
        P("gx", "gy", None),
        P(),
        P(None, "gx", None),
        P(None, None, "gx"),
        P(None, "gx", None),
        P(None, None, "gx"),
        P(),
    )
    out_specs = (P("gx", "gy", None), P("gx", "gy", None), P("gx", "gy", None))
    return jax.shard_map(local, mesh=mesh, in_specs=in_specs, out_specs=out_specs, check_vma=False)
```

```python
import jax
import jax.numpy as jnp
from jax import lax
from jax.sharding import PartitionSpec as P

NSWEEP = 3


PRECISE = lax.Precision.HIGHEST
WEIGHTS = (0.5, 0.5, 0.15, 0.15, 0.05, 0.05)
STORAGE = 0.1


def with_halo(array, sides, width):
    for axis, dim in sides:
        peers, length = (lax.axis_size(axis), array.shape[dim])
        up = [(i, (i + 1) % peers) for i in range(peers - 1)]
        down = [(j, i) for i, j in up]
        last = lax.slice_in_dim(array, length - width, length, axis=dim)
        leading = lax.slice_in_dim(array, 0, width, axis=dim)
        before = lax.ppermute(last, axis, up)
        after = lax.ppermute(leading, axis, down)
        array = jnp.concatenate([before, array, after], axis=dim)
    return array


def neighbours(padded):
    return [
        padded[:-2, 1:-1, 1:-1],
        padded[2:, 1:-1, 1:-1],
        padded[1:-1, :-2, 1:-1],
        padded[1:-1, 2:, 1:-1],
        padded[1:-1, 1:-1, :-2],
        padded[1:-1, 1:-1, 2:],
    ]


def face_terms(padded):
    centre = padded[1:-1, 1:-1, 1:-1]
    return [
        weight * 2.0 * centre * beside / (centre + beside)
        for weight, beside in zip(WEIGHTS, neighbours(padded))
    ]


def apply_operator(padded, face_list):
    centre = padded[1:-1, 1:-1, 1:-1]
    result_sum = STORAGE * centre
    for face_term, beside in zip(face_list, neighbours(padded)):
        result_sum = result_sum + face_term * (centre - beside)
    return result_sum


def padded_depth(field_now):
    return jnp.pad(field_now, ((0, 0), (0, 0), (1, 1)))


def chain_solve(chain_rows):
    blocks_count = chain_rows.shape[0]
    carry_value = jnp.zeros_like(chain_rows[0, 0])
    carry_gain = jnp.zeros_like(chain_rows[0, 0])
    first_parts, first_links, last_parts, last_links = ([], [], [], [])
    for block_index in range(blocks_count):
        pivot_value = 1.0 - chain_rows[block_index, 2] * carry_gain
        first_part = (
            chain_rows[block_index, 0] - chain_rows[block_index, 2] * carry_value
        ) / pivot_value
        first_link = chain_rows[block_index, 4] / pivot_value
        carry_value = (
            chain_rows[block_index, 1]
            - chain_rows[block_index, 3] * carry_value
            + chain_rows[block_index, 3] * carry_gain * first_part
        )
        carry_gain = (
            chain_rows[block_index, 5] + chain_rows[block_index, 3] * carry_gain * first_link
        )
        first_parts.append(first_part)
        first_links.append(first_link)
        last_parts.append(carry_value)
        last_links.append(carry_gain)
    following = jnp.zeros_like(carry_value)
    last_values = [following] * blocks_count
    next_values = [following] * blocks_count
    for block_index in range(blocks_count - 1, -1, -1):
        next_values[block_index] = following
        last_values[block_index] = last_parts[block_index] - last_links[block_index] * following
        following = first_parts[block_index] - first_links[block_index] * following
    previous = [jnp.zeros_like(following)] + last_values[:-1]
    return jnp.stack(
        [
            jnp.stack([previous[block_index], next_values[block_index]])
            for block_index in range(blocks_count)
        ]
    )


def reduced_solve(chain_local):
    peers = lax.axis_size("gx")
    packed = jnp.broadcast_to(chain_local[None], (peers,) + chain_local.shape)
    everyone = lax.all_to_all(packed, "gx", 0, 0, tiled=True)
    solved = chain_solve(everyone)
    return lax.dynamic_index_in_dim(solved, lax.axis_index("gx"), 0, keepdims=False)


def line_apply(grouped, matrices, couples):
    values = jnp.einsum("gic,cgm->igm", matrices, grouped, precision=PRECISE)
    group_count, column_count = (values.shape[1], values.shape[2])
    lower_couple = couples[0]
    upper_couple = couples[1]

    def spread(vector):
        return jnp.broadcast_to(vector[:, None], (group_count, column_count)).reshape(
            group_count * column_count
        )

    chain_local = jnp.stack(
        [
            values[0].reshape(-1),
            values[-1].reshape(-1),
            spread(lower_couple * matrices[:, 0, 0]),
            spread(lower_couple * matrices[:, -1, 0]),
            spread(upper_couple * matrices[:, 0, -1]),
            spread(upper_couple * matrices[:, -1, -1]),
        ]
    )
    solved = reduced_solve(chain_local)
    previous = solved[0].reshape(group_count, column_count)
    following = solved[1].reshape(group_count, column_count)
    first_column = jnp.transpose(matrices[:, :, 0])
    last_column = jnp.transpose(matrices[:, :, -1])
    return (
        values
        - (lower_couple[:, None] * previous)[None] * first_column[:, :, None]
        - (upper_couple[:, None] * following)[None] * last_column[:, :, None],
        previous,
        following,
    )


def row_apply(rows, matrix, couple_pair):
    values = jnp.einsum("mc,ic->mi", rows, matrix, precision=PRECISE)
    lower_couple = couple_pair[0]
    upper_couple = couple_pair[1]
    line_count = values.shape[0]

    def spread(value):
        return jnp.broadcast_to(value, (line_count,))

    chain_local = jnp.stack(
        [
            values[:, 0],
            values[:, -1],
            spread(lower_couple * matrix[0, 0]),
            spread(lower_couple * matrix[-1, 0]),
            spread(upper_couple * matrix[0, -1]),
            spread(upper_couple * matrix[-1, -1]),
        ]
    )
    solved = reduced_solve(chain_local)
    return (
        values
        - (lower_couple * solved[0])[:, None] * matrix[:, 0][None, :]
        - (upper_couple * solved[1])[:, None] * matrix[:, -1][None, :]
    )


def sorted_positions(layer_ids, layers, per_layer):
    depth_cells = layer_ids.shape[0]
    kinds = jnp.arange(layers, dtype=jnp.int32)
    onehot = (layer_ids[:, None] == kinds[None, :]).astype(jnp.int32)
    before = jnp.cumsum(onehot, axis=0) - onehot
    restore = jnp.sum(onehot * (before + kinds[None, :] * per_layer), axis=1)
    cells = jnp.arange(depth_cells, dtype=jnp.int32)
    order = jnp.sum(jnp.where(restore[None, :] == cells[:, None], cells[None, :], 0), axis=1)
    return order, restore


def local(
    source_field,
    permeability,
    layer_ids,
    inverse_fine,
    couple_fine,
    inverse_coarse,
    couple_coarse,
    owner_map,
):
    block_width, planes, depth_cells = source_field.shape
    layers = inverse_fine.shape[0]
    per_layer = depth_cells // layers
    order, restore = sorted_positions(layer_ids, layers, per_layer)
    halo_permeability = with_halo(permeability, (("gx", 0), ("gy", 1)), 1)
    face_list = face_terms(padded_depth(halo_permeability))
    rows = lax.axis_size("gy")
    up = [(i, i + 1) for i in range(rows - 1)]
    down = [(j, i) for i, j in up]

    def residual_of(field_now, left, right):
        lower = lax.ppermute(field_now[:, planes - 1 :, :], "gy", up)
        upper = lax.ppermute(field_now[:, :1, :], "gy", down)
        middle = jnp.concatenate([left, field_now, right], axis=0)
        padded = jnp.pad(middle, ((0, 0), (1, 1), (0, 0)))
        partial = source_field - apply_operator(padded_depth(padded), face_list)
        return (
            partial.at[:, :1, :]
            .add(face_list[2][:, :1, :] * lower)
            .at[:, planes - 1 :, :]
            .add(face_list[3][:, planes - 1 :, :] * upper)
        )

    line_count = planes * depth_cells
    lines_per_layer = planes * per_layer
    plane_of = jnp.arange(planes, dtype=jnp.int32)[:, None]
    line_restore = (
        (restore // per_layer)[None, :] * lines_per_layer
        + plane_of * per_layer
        + (restore % per_layer)[None, :]
    ).reshape(line_count)
    line_order = (
        plane_of[None, :, :] * depth_cells + order.reshape(layers, 1, per_layer)
    ).reshape(line_count)

    def unsorted(lines):
        return jnp.take(lines.reshape(line_count), line_restore, axis=0).reshape(
            1, planes, depth_cells
        )

    fine_couples = couple_fine[:, :, 0]
    solution = jnp.zeros_like(source_field)
    left = jnp.zeros_like(source_field[:1])
    right = jnp.zeros_like(source_field[:1])
    update = source_field
    for sweep_index in range(NSWEEP):
        if sweep_index > 0:
            update = residual_of(solution, left, right)
        ordered = jnp.take(update.reshape(block_width, line_count), line_order, axis=1)
        change, previous, following = line_apply(
            ordered.reshape(block_width, layers, lines_per_layer),
            inverse_fine,
            fine_couples,
        )
        solution = solution + jnp.take(
            change.reshape(block_width, line_count), line_restore, axis=1
        ).reshape(block_width, planes, depth_cells)
        left = left + unsorted(previous)
        right = right + unsorted(following)
    residual = residual_of(solution, left, right)
    coarse = 0.5 * (residual[:, 0::2, :] + residual[:, 1::2, :])
    groups = lax.axis_size("gy")
    position = lax.axis_index("gy")
    chunk = depth_cells // groups
    aggregates = 8
    owners = owner_map[:, 0]
    coarse_rows = jnp.take(jnp.transpose(coarse[:, 0, :]), order, axis=0)
    pieces = lax.all_to_all(
        coarse_rows.reshape(groups, chunk, block_width), "gy", 0, 0, tiled=True
    )
    member = (owners[:, None] == jnp.arange(aggregates, dtype=jnp.int32)[None, :]).astype(
        jnp.float32
    )
    summed = jnp.einsum("jzx,jo->ozx", pieces, member, precision=PRECISE)
    own_layer = (position * chunk) // per_layer
    matrix = lax.dynamic_index_in_dim(inverse_coarse, own_layer, 0, keepdims=False)
    couples = lax.dynamic_index_in_dim(couple_coarse[:, :, 0], own_layer, 1, keepdims=False)
    smoothed = row_apply(summed.reshape(aggregates * chunk, block_width), matrix, couples)
    outgoing = jnp.take(smoothed.reshape(aggregates, chunk, block_width), owners, axis=0)
    returned = lax.all_to_all(outgoing, "gy", 0, 0, tiled=True)
    result = jnp.take(returned.reshape(depth_cells, block_width), restore, axis=0)
    return (solution, residual, jnp.transpose(result)[:, None, :])


def solution(mesh):
    in_specs = (
        P("gx", "gy", None),
        P("gx", "gy", None),
        P(),
        P(None, "gx", None),
        P(None, None, "gx"),
        P(None, "gx", None),
        P(None, None, "gx"),
        P(),
    )
    out_specs = (P("gx", "gy", None), P("gx", "gy", None), P("gx", "gy", None))
    return jax.shard_map(local, mesh=mesh, in_specs=in_specs, out_specs=out_specs, check_vma=False)
```

```python
import jax
import jax.numpy as jnp
from jax import lax
from jax.sharding import PartitionSpec as P

NSWEEP = 3


PRECISE = lax.Precision.HIGHEST
WEIGHTS = (0.5, 0.5, 0.15, 0.15, 0.05, 0.05)
STORAGE = 0.1


def with_halo(array, sides, width):
    for axis, dim in sides:
        peers, length = (lax.axis_size(axis), array.shape[dim])
        up = [(i, (i + 1) % peers) for i in range(peers - 1)]
        down = [(j, i) for i, j in up]
        last = lax.slice_in_dim(array, length - width, length, axis=dim)
        leading = lax.slice_in_dim(array, 0, width, axis=dim)
        before = lax.ppermute(last, axis, up)
        after = lax.ppermute(leading, axis, down)
        array = jnp.concatenate([before, array, after], axis=dim)
    return array


def neighbours(padded):
    return [
        padded[:-2, 1:-1, 1:-1],
        padded[2:, 1:-1, 1:-1],
        padded[1:-1, :-2, 1:-1],
        padded[1:-1, 2:, 1:-1],
        padded[1:-1, 1:-1, :-2],
        padded[1:-1, 1:-1, 2:],
    ]


def face_terms(padded):
    centre = padded[1:-1, 1:-1, 1:-1]
    return [
        weight * 2.0 * centre * beside / (centre + beside)
        for weight, beside in zip(WEIGHTS, neighbours(padded))
    ]


def apply_operator(padded, face_list):
    centre = padded[1:-1, 1:-1, 1:-1]
    result_sum = STORAGE * centre
    for face_term, beside in zip(face_list, neighbours(padded)):
        result_sum = result_sum + face_term * (centre - beside)
    return result_sum


def padded_depth(field_now):
    return jnp.pad(field_now, ((0, 0), (0, 0), (1, 1)))


def chain_solve(chain_rows):
    blocks_count = chain_rows.shape[0]
    carry_value = jnp.zeros_like(chain_rows[0, 0])
    carry_gain = jnp.zeros_like(chain_rows[0, 0])
    first_parts, first_links, last_parts, last_links = ([], [], [], [])
    for block_index in range(blocks_count):
        pivot_value = 1.0 - chain_rows[block_index, 2] * carry_gain
        first_part = (
            chain_rows[block_index, 0] - chain_rows[block_index, 2] * carry_value
        ) / pivot_value
        first_link = chain_rows[block_index, 4] / pivot_value
        carry_value = (
            chain_rows[block_index, 1]
            - chain_rows[block_index, 3] * carry_value
            + chain_rows[block_index, 3] * carry_gain * first_part
        )
        carry_gain = (
            chain_rows[block_index, 5] + chain_rows[block_index, 3] * carry_gain * first_link
        )
        first_parts.append(first_part)
        first_links.append(first_link)
        last_parts.append(carry_value)
        last_links.append(carry_gain)
    following = jnp.zeros_like(carry_value)
    last_values = [following] * blocks_count
    next_values = [following] * blocks_count
    for block_index in range(blocks_count - 1, -1, -1):
        next_values[block_index] = following
        last_values[block_index] = last_parts[block_index] - last_links[block_index] * following
        following = first_parts[block_index] - first_links[block_index] * following
    previous = [jnp.zeros_like(following)] + last_values[:-1]
    return jnp.stack(
        [
            jnp.stack([previous[block_index], next_values[block_index]])
            for block_index in range(blocks_count)
        ]
    )


def reduced_solve(chain_local):
    peers = lax.axis_size("gx")
    packed = jnp.broadcast_to(chain_local[None], (peers,) + chain_local.shape)
    everyone = lax.all_to_all(packed, "gx", 0, 0, tiled=True)
    solved = chain_solve(everyone)
    return lax.dynamic_index_in_dim(solved, lax.axis_index("gx"), 0, keepdims=False)


def line_apply(grouped, matrices, couples):
    values = jnp.einsum("gic,cgm->igm", matrices, grouped, precision=lax.Precision.HIGH)
    group_count, column_count = (values.shape[1], values.shape[2])
    lower_couple = couples[0]
    upper_couple = couples[1]

    def spread(vector):
        return jnp.broadcast_to(vector[:, None], (group_count, column_count)).reshape(
            group_count * column_count
        )

    chain_local = jnp.stack(
        [
            values[0].reshape(-1),
            values[-1].reshape(-1),
            spread(lower_couple * matrices[:, 0, 0]),
            spread(lower_couple * matrices[:, -1, 0]),
            spread(upper_couple * matrices[:, 0, -1]),
            spread(upper_couple * matrices[:, -1, -1]),
        ]
    )
    solved = reduced_solve(chain_local)
    previous = solved[0].reshape(group_count, column_count)
    following = solved[1].reshape(group_count, column_count)
    first_column = jnp.transpose(matrices[:, :, 0])
    last_column = jnp.transpose(matrices[:, :, -1])
    return (
        values
        - (lower_couple[:, None] * previous)[None] * first_column[:, :, None]
        - (upper_couple[:, None] * following)[None] * last_column[:, :, None],
        previous,
        following,
    )


def row_apply(rows, matrix, couple_pair):
    values = jnp.einsum("mc,ic->mi", rows, matrix, precision=lax.Precision.HIGH)
    lower_couple = couple_pair[0]
    upper_couple = couple_pair[1]
    line_count = values.shape[0]

    def spread(value):
        return jnp.broadcast_to(value, (line_count,))

    chain_local = jnp.stack(
        [
            values[:, 0],
            values[:, -1],
            spread(lower_couple * matrix[0, 0]),
            spread(lower_couple * matrix[-1, 0]),
            spread(upper_couple * matrix[0, -1]),
            spread(upper_couple * matrix[-1, -1]),
        ]
    )
    solved = reduced_solve(chain_local)
    return (
        values
        - (lower_couple * solved[0])[:, None] * matrix[:, 0][None, :]
        - (upper_couple * solved[1])[:, None] * matrix[:, -1][None, :]
    )


def sorted_positions(layer_ids, layers, per_layer):
    depth_cells = layer_ids.shape[0]
    kinds = jnp.arange(layers, dtype=jnp.int32)
    onehot = (layer_ids[:, None] == kinds[None, :]).astype(jnp.int32)
    before = jnp.cumsum(onehot, axis=0) - onehot
    restore = jnp.sum(onehot * (before + kinds[None, :] * per_layer), axis=1)
    cells = jnp.arange(depth_cells, dtype=jnp.int32)
    order = jnp.sum(jnp.where(restore[None, :] == cells[:, None], cells[None, :], 0), axis=1)
    return order, restore


def local(
    source_field,
    permeability,
    layer_ids,
    inverse_fine,
    couple_fine,
    inverse_coarse,
    couple_coarse,
    owner_map,
):
    block_width, planes, depth_cells = source_field.shape
    layers = inverse_fine.shape[0]
    per_layer = depth_cells // layers
    order, restore = sorted_positions(layer_ids, layers, per_layer)
    halo_permeability = with_halo(permeability, (("gx", 0), ("gy", 1)), 1)
    face_list = face_terms(padded_depth(halo_permeability))
    rows = lax.axis_size("gy")
    up = [(i, i + 1) for i in range(rows - 1)]
    down = [(j, i) for i, j in up]

    def residual_of(field_now, left, right):
        lower = lax.ppermute(field_now[:, planes - 1 :, :], "gy", up)
        upper = lax.ppermute(field_now[:, :1, :], "gy", down)
        middle = jnp.concatenate([left, field_now, right], axis=0)
        padded = jnp.pad(middle, ((0, 0), (1, 1), (0, 0)))
        partial = source_field - apply_operator(padded_depth(padded), face_list)
        return (
            partial.at[:, :1, :]
            .add(face_list[2][:, :1, :] * lower)
            .at[:, planes - 1 :, :]
            .add(face_list[3][:, planes - 1 :, :] * upper)
        )

    def unsorted(lines):
        shaped = jnp.transpose(lines.reshape(layers, planes, per_layer), (1, 0, 2))
        return jnp.take(shaped.reshape(planes, depth_cells), restore, axis=1)[None]

    fine_couples = couple_fine[:, :, 0]
    solution = jnp.zeros_like(source_field)
    left = jnp.zeros_like(source_field[:1])
    right = jnp.zeros_like(source_field[:1])
    update = source_field
    for sweep_index in range(NSWEEP):
        if sweep_index > 0:
            update = residual_of(solution, left, right)
        ordered = jnp.take(update, order, axis=2).reshape(block_width, planes, layers, per_layer)
        change, previous, following = line_apply(
            jnp.transpose(ordered, (0, 2, 1, 3)).reshape(block_width, layers, planes * per_layer),
            inverse_fine,
            fine_couples,
        )
        from_shaped = jnp.transpose(
            change.reshape(block_width, layers, planes, per_layer), (0, 2, 1, 3)
        )
        solution = solution + jnp.take(
            from_shaped.reshape(block_width, planes, depth_cells), restore, axis=2
        )
        left = left + unsorted(previous)
        right = right + unsorted(following)
    residual = residual_of(solution, left, right)
    coarse = 0.5 * (residual[:, 0::2, :] + residual[:, 1::2, :])
    groups = lax.axis_size("gy")
    position = lax.axis_index("gy")
    chunk = depth_cells // groups
    aggregates = 8
    owners = owner_map[:, 0]
    coarse_rows = jnp.take(jnp.transpose(coarse[:, 0, :]), order, axis=0)
    pieces = lax.all_to_all(
        coarse_rows.reshape(groups, chunk, block_width), "gy", 0, 0, tiled=True
    )
    member = (owners[:, None] == jnp.arange(aggregates, dtype=jnp.int32)[None, :]).astype(
        jnp.float32
    )
    summed = jnp.einsum("jzx,jo->ozx", pieces, member, precision=PRECISE)
    own_layer = (position * chunk) // per_layer
    matrix = lax.dynamic_index_in_dim(inverse_coarse, own_layer, 0, keepdims=False)
    couples = lax.dynamic_index_in_dim(couple_coarse[:, :, 0], own_layer, 1, keepdims=False)
    smoothed = row_apply(summed.reshape(aggregates * chunk, block_width), matrix, couples)
    outgoing = jnp.take(smoothed.reshape(aggregates, chunk, block_width), owners, axis=0)
    returned = lax.all_to_all(outgoing, "gy", 0, 0, tiled=True)
    result = jnp.take(returned.reshape(depth_cells, block_width), restore, axis=0)
    return (solution, residual, jnp.transpose(result)[:, None, :])


def solution(mesh):
    in_specs = (
        P("gx", "gy", None),
        P("gx", "gy", None),
        P(),
        P(None, "gx", None),
        P(None, None, "gx"),
        P(None, "gx", None),
        P(None, None, "gx"),
        P(),
    )
    out_specs = (P("gx", "gy", None), P("gx", "gy", None), P("gx", "gy", None))
    return jax.shard_map(local, mesh=mesh, in_specs=in_specs, out_specs=out_specs, check_vma=False)
```

```python
import jax
import jax.numpy as jnp
from jax import lax
from jax.sharding import PartitionSpec as P

NSWEEP = 3


PRECISE = lax.Precision.HIGHEST
WEIGHTS = (0.5, 0.5, 0.15, 0.15, 0.05, 0.05)
STORAGE = 0.1


def with_halo(array, sides, width):
    for axis, dim in sides:
        peers, length = (lax.axis_size(axis), array.shape[dim])
        up = [(i, (i + 1) % peers) for i in range(peers - 1)]
        down = [(j, i) for i, j in up]
        last = lax.slice_in_dim(array, length - width, length, axis=dim)
        leading = lax.slice_in_dim(array, 0, width, axis=dim)
        before = lax.ppermute(last, axis, up)
        after = lax.ppermute(leading, axis, down)
        array = jnp.concatenate([before, array, after], axis=dim)
    return array


def neighbours(padded):
    return [
        padded[:-2, 1:-1, 1:-1],
        padded[2:, 1:-1, 1:-1],
        padded[1:-1, :-2, 1:-1],
        padded[1:-1, 2:, 1:-1],
        padded[1:-1, 1:-1, :-2],
        padded[1:-1, 1:-1, 2:],
    ]


def face_terms(padded):
    centre = padded[1:-1, 1:-1, 1:-1]
    return [
        weight * 2.0 * centre * beside / (centre + beside)
        for weight, beside in zip(WEIGHTS, neighbours(padded))
    ]


def apply_operator(padded, face_list):
    centre = padded[1:-1, 1:-1, 1:-1]
    result_sum = STORAGE * centre
    for face_term, beside in zip(face_list, neighbours(padded)):
        result_sum = result_sum + face_term * (centre - beside)
    return result_sum


def padded_depth(field_now):
    return jnp.pad(field_now, ((0, 0), (0, 0), (1, 1)))


def chain_solve(chain_rows):
    blocks_count = chain_rows.shape[0]
    carry_value = jnp.zeros_like(chain_rows[0, 0])
    carry_gain = jnp.zeros_like(chain_rows[0, 0])
    first_parts, first_links, last_parts, last_links = ([], [], [], [])
    for block_index in range(blocks_count):
        pivot_value = 1.0 - chain_rows[block_index, 2] * carry_gain
        first_part = (
            chain_rows[block_index, 0] - chain_rows[block_index, 2] * carry_value
        ) / pivot_value
        first_link = chain_rows[block_index, 4] / pivot_value
        carry_value = (
            chain_rows[block_index, 1]
            - chain_rows[block_index, 3] * carry_value
            + chain_rows[block_index, 3] * carry_gain * first_part
        )
        carry_gain = (
            chain_rows[block_index, 5] + chain_rows[block_index, 3] * carry_gain * first_link
        )
        first_parts.append(first_part)
        first_links.append(first_link)
        last_parts.append(carry_value)
        last_links.append(carry_gain)
    following = jnp.zeros_like(carry_value)
    last_values = [following] * blocks_count
    next_values = [following] * blocks_count
    for block_index in range(blocks_count - 1, -1, -1):
        next_values[block_index] = following
        last_values[block_index] = last_parts[block_index] - last_links[block_index] * following
        following = first_parts[block_index] - first_links[block_index] * following
    previous = [jnp.zeros_like(following)] + last_values[:-1]
    return jnp.stack(
        [
            jnp.stack([previous[block_index], next_values[block_index]])
            for block_index in range(blocks_count)
        ]
    )


def reduced_solve(chain_local):
    peers = lax.axis_size("gx")
    packed = jnp.broadcast_to(chain_local[None], (peers,) + chain_local.shape)
    everyone = lax.all_to_all(packed, "gx", 0, 0, tiled=True)
    solved = chain_solve(everyone)
    return lax.dynamic_index_in_dim(solved, lax.axis_index("gx"), 0, keepdims=False)


def line_apply(grouped, matrices, couples):
    values = jnp.einsum("gic,cgm->igm", matrices, grouped, precision=PRECISE)
    group_count, column_count = (values.shape[1], values.shape[2])
    lower_couple = couples[0]
    upper_couple = couples[1]

    def spread(vector):
        return jnp.broadcast_to(vector[:, None], (group_count, column_count)).reshape(
            group_count * column_count
        )

    chain_local = jnp.stack(
        [
            values[0].reshape(-1),
            values[-1].reshape(-1),
            spread(lower_couple * matrices[:, 0, 0]),
            spread(lower_couple * matrices[:, -1, 0]),
            spread(upper_couple * matrices[:, 0, -1]),
            spread(upper_couple * matrices[:, -1, -1]),
        ]
    )
    solved = reduced_solve(chain_local)
    previous = solved[0].reshape(group_count, column_count)
    following = solved[1].reshape(group_count, column_count)
    first_column = jnp.transpose(matrices[:, :, 0])
    last_column = jnp.transpose(matrices[:, :, -1])
    return (
        values
        - (lower_couple[:, None] * previous)[None] * first_column[:, :, None]
        - (upper_couple[:, None] * following)[None] * last_column[:, :, None],
        previous,
        following,
    )


def row_apply(rows, matrix, couple_pair):
    values = jnp.einsum("mc,ic->mi", rows, matrix, precision=PRECISE)
    lower_couple = couple_pair[0]
    upper_couple = couple_pair[1]
    line_count = values.shape[0]

    def spread(value):
        return jnp.broadcast_to(value, (line_count,))

    chain_local = jnp.stack(
        [
            values[:, 0],
            values[:, -1],
            spread(lower_couple * matrix[0, 0]),
            spread(lower_couple * matrix[-1, 0]),
            spread(upper_couple * matrix[0, -1]),
            spread(upper_couple * matrix[-1, -1]),
        ]
    )
    solved = reduced_solve(chain_local)
    return (
        values
        - (lower_couple * solved[0])[:, None] * matrix[:, 0][None, :]
        - (upper_couple * solved[1])[:, None] * matrix[:, -1][None, :]
    )


def sorted_positions(layer_ids, layers, per_layer):
    depth_cells = layer_ids.shape[0]
    kinds = jnp.arange(layers, dtype=jnp.int32)
    onehot = (layer_ids[:, None] == kinds[None, :]).astype(jnp.int32)
    before = jnp.cumsum(onehot, axis=0) - onehot
    restore = jnp.sum(onehot * (before + kinds[None, :] * per_layer), axis=1)
    cells = jnp.arange(depth_cells, dtype=jnp.int32)
    order = jnp.sum(jnp.where(restore[None, :] == cells[:, None], cells[None, :], 0), axis=1)
    return order, restore


def local(
    source_field,
    permeability,
    layer_ids,
    inverse_fine,
    couple_fine,
    inverse_coarse,
    couple_coarse,
    owner_map,
):
    block_width, planes, depth_cells = source_field.shape
    layers = inverse_fine.shape[0]
    per_layer = depth_cells // layers
    order, restore = sorted_positions(layer_ids, layers, per_layer)
    halo_permeability = with_halo(permeability, (("gx", 0),), 1)
    face_list = face_terms(padded_depth(jnp.pad(halo_permeability, ((0, 0), (1, 1), (0, 0)))))
    rows = lax.axis_size("gy")
    up = [(i, i + 1) for i in range(rows - 1)]
    down = [(j, i) for i, j in up]

    def off_face(centre, beside):
        return WEIGHTS[2] * 2.0 * centre * beside / (centre + beside)

    def residual_of(field_now, left, right, faces_y):
        send_up = field_now[:, planes - 1 :, :]
        send_down = field_now[:, :1, :]
        if faces_y is None:
            send_up = jnp.concatenate([send_up, permeability[:, planes - 1 :, :]], axis=1)
            send_down = jnp.concatenate([send_down, permeability[:, :1, :]], axis=1)
        got_lower = lax.ppermute(send_up, "gy", up)
        got_upper = lax.ppermute(send_down, "gy", down)
        if faces_y is None:
            faces_y = (
                off_face(permeability[:, :1, :], got_lower[:, 1:, :]),
                off_face(permeability[:, planes - 1 :, :], got_upper[:, 1:, :]),
            )
        middle = jnp.concatenate([left, field_now, right], axis=0)
        padded = jnp.pad(middle, ((0, 0), (1, 1), (0, 0)))
        partial = source_field - apply_operator(padded_depth(padded), face_list)
        result = partial.at[:, :1, :].add(
            faces_y[0] * (got_lower[:, :1, :] - field_now[:, :1, :])
        )
        result = result.at[:, planes - 1 :, :].add(
            faces_y[1] * (got_upper[:, :1, :] - field_now[:, planes - 1 :, :])
        )
        return result, faces_y

    def unsorted(lines):
        shaped = jnp.transpose(lines.reshape(layers, planes, per_layer), (1, 0, 2))
        return jnp.take(shaped.reshape(planes, depth_cells), restore, axis=1)[None]

    fine_couples = couple_fine[:, :, 0]
    solution = jnp.zeros_like(source_field)
    left = jnp.zeros_like(source_field[:1])
    right = jnp.zeros_like(source_field[:1])
    update = source_field
    faces_y = None
    for sweep_index in range(NSWEEP):
        if sweep_index > 0:
            update, faces_y = residual_of(solution, left, right, faces_y)
        ordered = jnp.take(update, order, axis=2).reshape(block_width, planes, layers, per_layer)
        change, previous, following = line_apply(
            jnp.transpose(ordered, (0, 2, 1, 3)).reshape(block_width, layers, planes * per_layer),
            inverse_fine,
            fine_couples,
        )
        from_shaped = jnp.transpose(
            change.reshape(block_width, layers, planes, per_layer), (0, 2, 1, 3)
        )
        solution = solution + jnp.take(
            from_shaped.reshape(block_width, planes, depth_cells), restore, axis=2
        )
        left = left + unsorted(previous)
        right = right + unsorted(following)
    residual, faces_y = residual_of(solution, left, right, faces_y)
    coarse = 0.5 * (residual[:, 0::2, :] + residual[:, 1::2, :])
    groups = lax.axis_size("gy")
    position = lax.axis_index("gy")
    chunk = depth_cells // groups
    aggregates = 8
    owners = owner_map[:, 0]
    coarse_rows = jnp.take(jnp.transpose(coarse[:, 0, :]), order, axis=0)
    pieces = lax.all_to_all(
        coarse_rows.reshape(groups, chunk, block_width), "gy", 0, 0, tiled=True
    )
    member = (owners[:, None] == jnp.arange(aggregates, dtype=jnp.int32)[None, :]).astype(
        jnp.float32
    )
    summed = jnp.einsum("jzx,jo->ozx", pieces, member, precision=PRECISE)
    own_layer = (position * chunk) // per_layer
    matrix = lax.dynamic_index_in_dim(inverse_coarse, own_layer, 0, keepdims=False)
    couples = lax.dynamic_index_in_dim(couple_coarse[:, :, 0], own_layer, 1, keepdims=False)
    smoothed = row_apply(summed.reshape(aggregates * chunk, block_width), matrix, couples)
    outgoing = jnp.take(smoothed.reshape(aggregates, chunk, block_width), owners, axis=0)
    returned = lax.all_to_all(outgoing, "gy", 0, 0, tiled=True)
    result = jnp.take(returned.reshape(depth_cells, block_width), restore, axis=0)
    return (solution, residual, jnp.transpose(result)[:, None, :])


def solution(mesh):
    in_specs = (
        P("gx", "gy", None),
        P("gx", "gy", None),
        P(),
        P(None, "gx", None),
        P(None, None, "gx"),
        P(None, "gx", None),
        P(None, None, "gx"),
        P(),
    )
    out_specs = (P("gx", "gy", None), P("gx", "gy", None), P("gx", "gy", None))
    return jax.shard_map(local, mesh=mesh, in_specs=in_specs, out_specs=out_specs, check_vma=False)
```

```python
import jax
import jax.numpy as jnp
from jax import lax
from jax.sharding import PartitionSpec as P

NSWEEP = 3


PRECISE = lax.Precision.HIGHEST
WEIGHTS = (0.5, 0.5, 0.15, 0.15, 0.05, 0.05)
STORAGE = 0.1


def with_halo(array, sides, width):
    for axis, dim in sides:
        peers, length = (lax.axis_size(axis), array.shape[dim])
        up = [(i, (i + 1) % peers) for i in range(peers - 1)]
        down = [(j, i) for i, j in up]
        last = lax.slice_in_dim(array, length - width, length, axis=dim)
        leading = lax.slice_in_dim(array, 0, width, axis=dim)
        before = lax.ppermute(last, axis, up)
        after = lax.ppermute(leading, axis, down)
        array = jnp.concatenate([before, array, after], axis=dim)
    return array


def neighbours(padded):
    return [
        padded[:-2, 1:-1, 1:-1],
        padded[2:, 1:-1, 1:-1],
        padded[1:-1, :-2, 1:-1],
        padded[1:-1, 2:, 1:-1],
        padded[1:-1, 1:-1, :-2],
        padded[1:-1, 1:-1, 2:],
    ]


def face_terms(padded):
    centre = padded[1:-1, 1:-1, 1:-1]
    return [
        weight * 2.0 * centre * beside / (centre + beside)
        for weight, beside in zip(WEIGHTS, neighbours(padded))
    ]


def apply_operator(padded, face_list):
    centre = padded[1:-1, 1:-1, 1:-1]
    result_sum = STORAGE * centre
    for face_term, beside in zip(face_list, neighbours(padded)):
        result_sum = result_sum + face_term * (centre - beside)
    return result_sum


def padded_depth(field_now):
    return jnp.pad(field_now, ((0, 0), (0, 0), (1, 1)))


def chain_solve(chain_rows):
    blocks_count = chain_rows.shape[0]
    carry_value = jnp.zeros_like(chain_rows[0, 0])
    carry_gain = jnp.zeros_like(chain_rows[0, 0])
    first_parts, first_links, last_parts, last_links = ([], [], [], [])
    for block_index in range(blocks_count):
        pivot_value = 1.0 - chain_rows[block_index, 2] * carry_gain
        first_part = (
            chain_rows[block_index, 0] - chain_rows[block_index, 2] * carry_value
        ) / pivot_value
        first_link = chain_rows[block_index, 4] / pivot_value
        carry_value = (
            chain_rows[block_index, 1]
            - chain_rows[block_index, 3] * carry_value
            + chain_rows[block_index, 3] * carry_gain * first_part
        )
        carry_gain = (
            chain_rows[block_index, 5] + chain_rows[block_index, 3] * carry_gain * first_link
        )
        first_parts.append(first_part)
        first_links.append(first_link)
        last_parts.append(carry_value)
        last_links.append(carry_gain)
    following = jnp.zeros_like(carry_value)
    last_values = [following] * blocks_count
    next_values = [following] * blocks_count
    for block_index in range(blocks_count - 1, -1, -1):
        next_values[block_index] = following
        last_values[block_index] = last_parts[block_index] - last_links[block_index] * following
        following = first_parts[block_index] - first_links[block_index] * following
    previous = [jnp.zeros_like(following)] + last_values[:-1]
    return jnp.stack(
        [
            jnp.stack([previous[block_index], next_values[block_index]])
            for block_index in range(blocks_count)
        ]
    )


def reduced_solve(chain_local):
    peers = lax.axis_size("gx")
    packed = jnp.broadcast_to(chain_local[None], (peers,) + chain_local.shape)
    everyone = lax.all_to_all(packed, "gx", 0, 0, tiled=True)
    solved = chain_solve(everyone)
    return lax.dynamic_index_in_dim(solved, lax.axis_index("gx"), 0, keepdims=False)


def line_apply(grouped, matrices, couples):
    values = jnp.einsum("gic,cgm->igm", matrices, grouped, precision=PRECISE)
    group_count, column_count = (values.shape[1], values.shape[2])
    lower_couple = couples[0]
    upper_couple = couples[1]

    def spread(vector):
        return jnp.broadcast_to(vector[:, None], (group_count, column_count)).reshape(
            group_count * column_count
        )

    chain_local = jnp.stack(
        [
            values[0].reshape(-1),
            values[-1].reshape(-1),
            spread(lower_couple * matrices[:, 0, 0]),
            spread(lower_couple * matrices[:, -1, 0]),
            spread(upper_couple * matrices[:, 0, -1]),
            spread(upper_couple * matrices[:, -1, -1]),
        ]
    )
    solved = reduced_solve(chain_local)
    previous = solved[0].reshape(group_count, column_count)
    following = solved[1].reshape(group_count, column_count)
    first_column = jnp.transpose(matrices[:, :, 0])
    last_column = jnp.transpose(matrices[:, :, -1])
    return (
        values
        - (lower_couple[:, None] * previous)[None] * first_column[:, :, None]
        - (upper_couple[:, None] * following)[None] * last_column[:, :, None],
        previous,
        following,
    )


def row_apply(rows, matrix, couple_pair):
    values = jnp.einsum("mc,ic->mi", rows, matrix, precision=PRECISE)
    lower_couple = couple_pair[0]
    upper_couple = couple_pair[1]
    line_count = values.shape[0]

    def spread(value):
        return jnp.broadcast_to(value, (line_count,))

    chain_local = jnp.stack(
        [
            values[:, 0],
            values[:, -1],
            spread(lower_couple * matrix[0, 0]),
            spread(lower_couple * matrix[-1, 0]),
            spread(upper_couple * matrix[0, -1]),
            spread(upper_couple * matrix[-1, -1]),
        ]
    )
    solved = reduced_solve(chain_local)
    return (
        values
        - (lower_couple * solved[0])[:, None] * matrix[:, 0][None, :]
        - (upper_couple * solved[1])[:, None] * matrix[:, -1][None, :]
    )


def sorted_positions(layer_ids, layers, per_layer):
    depth_cells = layer_ids.shape[0]
    kinds = jnp.arange(layers, dtype=jnp.int32)
    onehot = (layer_ids[:, None] == kinds[None, :]).astype(jnp.int32)
    before = jnp.cumsum(onehot, axis=0) - onehot
    restore = jnp.sum(onehot * (before + kinds[None, :] * per_layer), axis=1)
    cells = jnp.arange(depth_cells, dtype=jnp.int32)
    order = jnp.sum(jnp.where(restore[None, :] == cells[:, None], cells[None, :], 0), axis=1)
    return order, restore


def local(
    source_field,
    permeability,
    layer_ids,
    inverse_fine,
    couple_fine,
    inverse_coarse,
    couple_coarse,
    owner_map,
):
    block_width, planes, depth_cells = source_field.shape
    layers = inverse_fine.shape[0]
    per_layer = depth_cells // layers
    order, restore = sorted_positions(layer_ids, layers, per_layer)
    halo_permeability = with_halo(permeability, (("gx", 0),), 1)
    face_list = face_terms(padded_depth(jnp.pad(halo_permeability, ((0, 0), (1, 1), (0, 0)))))
    rows = lax.axis_size("gy")
    up = [(i, i + 1) for i in range(rows - 1)]
    down = [(j, i) for i, j in up]

    def off_face(centre, beside):
        return WEIGHTS[2] * 2.0 * centre * beside / (centre + beside)

    def residual_of(field_now, left, right, faces_y):
        send_up = field_now[:, planes - 1 :, :]
        send_down = field_now[:, :1, :]
        if faces_y is None:
            send_up = jnp.concatenate([send_up, permeability[:, planes - 1 :, :]], axis=1)
            send_down = jnp.concatenate([send_down, permeability[:, :1, :]], axis=1)
        got_lower = lax.ppermute(send_up, "gy", up)
        got_upper = lax.ppermute(send_down, "gy", down)
        if faces_y is None:
            faces_y = (
                off_face(permeability[:, :1, :], got_lower[:, 1:, :]),
                off_face(permeability[:, planes - 1 :, :], got_upper[:, 1:, :]),
            )
        middle = jnp.concatenate([left, field_now, right], axis=0)
        padded = jnp.pad(middle, ((0, 0), (1, 1), (0, 0)))
        partial = source_field - apply_operator(padded_depth(padded), face_list)
        low_part = faces_y[0] * (got_lower[:, :1, :] - field_now[:, :1, :])
        high_part = faces_y[1] * (got_upper[:, :1, :] - field_now[:, planes - 1 :, :])
        if planes == 1:
            correction = low_part + high_part
        else:
            inner = jnp.zeros_like(field_now[:, 1 : planes - 1, :])
            correction = jnp.concatenate([low_part, inner, high_part], axis=1)
        return partial + correction, faces_y

    def unsorted(lines):
        shaped = jnp.transpose(lines.reshape(layers, planes, per_layer), (1, 0, 2))
        return jnp.take(shaped.reshape(planes, depth_cells), restore, axis=1)[None]

    fine_couples = couple_fine[:, :, 0]
    solution = jnp.zeros_like(source_field)
    left = jnp.zeros_like(source_field[:1])
    right = jnp.zeros_like(source_field[:1])
    update = source_field
    faces_y = None
    for sweep_index in range(NSWEEP):
        if sweep_index > 0:
            update, faces_y = residual_of(solution, left, right, faces_y)
        ordered = jnp.take(update, order, axis=2).reshape(block_width, planes, layers, per_layer)
        change, previous, following = line_apply(
            jnp.transpose(ordered, (0, 2, 1, 3)).reshape(block_width, layers, planes * per_layer),
            inverse_fine,
            fine_couples,
        )
        from_shaped = jnp.transpose(
            change.reshape(block_width, layers, planes, per_layer), (0, 2, 1, 3)
        )
        solution = solution + jnp.take(
            from_shaped.reshape(block_width, planes, depth_cells), restore, axis=2
        )
        left = left + unsorted(previous)
        right = right + unsorted(following)
    residual, faces_y = residual_of(solution, left, right, faces_y)
    coarse = 0.5 * (residual[:, 0::2, :] + residual[:, 1::2, :])
    groups = lax.axis_size("gy")
    position = lax.axis_index("gy")
    chunk = depth_cells // groups
    aggregates = 8
    owners = owner_map[:, 0]
    coarse_rows = jnp.take(jnp.transpose(coarse[:, 0, :]), order, axis=0)
    pieces = lax.all_to_all(
        coarse_rows.reshape(groups, chunk, block_width), "gy", 0, 0, tiled=True
    )
    member = (owners[:, None] == jnp.arange(aggregates, dtype=jnp.int32)[None, :]).astype(
        jnp.float32
    )
    summed = jnp.einsum("jzx,jo->ozx", pieces, member, precision=PRECISE)
    own_layer = (position * chunk) // per_layer
    matrix = lax.dynamic_index_in_dim(inverse_coarse, own_layer, 0, keepdims=False)
    couples = lax.dynamic_index_in_dim(couple_coarse[:, :, 0], own_layer, 1, keepdims=False)
    smoothed = row_apply(summed.reshape(aggregates * chunk, block_width), matrix, couples)
    outgoing = jnp.take(smoothed.reshape(aggregates, chunk, block_width), owners, axis=0)
    returned = lax.all_to_all(outgoing, "gy", 0, 0, tiled=True)
    result = jnp.take(returned.reshape(depth_cells, block_width), restore, axis=0)
    return (solution, residual, jnp.transpose(result)[:, None, :])


def solution(mesh):
    in_specs = (
        P("gx", "gy", None),
        P("gx", "gy", None),
        P(),
        P(None, "gx", None),
        P(None, None, "gx"),
        P(None, "gx", None),
        P(None, None, "gx"),
        P(),
    )
    out_specs = (P("gx", "gy", None), P("gx", "gy", None), P("gx", "gy", None))
    return jax.shard_map(local, mesh=mesh, in_specs=in_specs, out_specs=out_specs, check_vma=False)
```

```python
import jax
import jax.numpy as jnp
from jax import lax
from jax.sharding import PartitionSpec as P

NSWEEP = 3


PRECISE = lax.Precision.HIGHEST
WEIGHTS = (0.5, 0.5, 0.15, 0.15, 0.05, 0.05)
STORAGE = 0.1


def with_halo(array, sides, width):
    for axis, dim in sides:
        peers, length = (lax.axis_size(axis), array.shape[dim])
        up = [(i, (i + 1) % peers) for i in range(peers - 1)]
        down = [(j, i) for i, j in up]
        last = lax.slice_in_dim(array, length - width, length, axis=dim)
        leading = lax.slice_in_dim(array, 0, width, axis=dim)
        before = lax.ppermute(last, axis, up)
        after = lax.ppermute(leading, axis, down)
        array = jnp.concatenate([before, array, after], axis=dim)
    return array


def neighbours(padded):
    return [
        padded[:-2, 1:-1, 1:-1],
        padded[2:, 1:-1, 1:-1],
        padded[1:-1, :-2, 1:-1],
        padded[1:-1, 2:, 1:-1],
        padded[1:-1, 1:-1, :-2],
        padded[1:-1, 1:-1, 2:],
    ]


def face_terms(padded):
    centre = padded[1:-1, 1:-1, 1:-1]
    return [
        weight * 2.0 * centre * beside / (centre + beside)
        for weight, beside in zip(WEIGHTS, neighbours(padded))
    ]


def apply_operator(padded, face_list):
    centre = padded[1:-1, 1:-1, 1:-1]
    result_sum = STORAGE * centre
    for face_term, beside in zip(face_list, neighbours(padded)):
        result_sum = result_sum + face_term * (centre - beside)
    return result_sum


def padded_depth(field_now):
    return jnp.pad(field_now, ((0, 0), (0, 0), (1, 1)))


def chain_solve(chain_rows):
    blocks_count = chain_rows.shape[0]
    carry_value = jnp.zeros_like(chain_rows[0, 0])
    carry_gain = jnp.zeros_like(chain_rows[0, 0])
    first_parts, first_links, last_parts, last_links = ([], [], [], [])
    for block_index in range(blocks_count):
        pivot_value = 1.0 - chain_rows[block_index, 2] * carry_gain
        first_part = (
            chain_rows[block_index, 0] - chain_rows[block_index, 2] * carry_value
        ) / pivot_value
        first_link = chain_rows[block_index, 4] / pivot_value
        carry_value = (
            chain_rows[block_index, 1]
            - chain_rows[block_index, 3] * carry_value
            + chain_rows[block_index, 3] * carry_gain * first_part
        )
        carry_gain = (
            chain_rows[block_index, 5] + chain_rows[block_index, 3] * carry_gain * first_link
        )
        first_parts.append(first_part)
        first_links.append(first_link)
        last_parts.append(carry_value)
        last_links.append(carry_gain)
    following = jnp.zeros_like(carry_value)
    last_values = [following] * blocks_count
    next_values = [following] * blocks_count
    for block_index in range(blocks_count - 1, -1, -1):
        next_values[block_index] = following
        last_values[block_index] = last_parts[block_index] - last_links[block_index] * following
        following = first_parts[block_index] - first_links[block_index] * following
    previous = [jnp.zeros_like(following)] + last_values[:-1]
    return jnp.stack(
        [
            jnp.stack([previous[block_index], next_values[block_index]])
            for block_index in range(blocks_count)
        ]
    )


def exchange(rows):
    peers = lax.axis_size("gx")
    packed = jnp.broadcast_to(rows[None], (peers,) + rows.shape)
    return lax.all_to_all(packed, "gx", 0, 0, tiled=True)


def reduced_solve(chain_local, known=None):
    everyone = exchange(chain_local)
    if known is not None:
        everyone = jnp.concatenate([everyone, known], axis=1)
    solved = chain_solve(everyone)
    return lax.dynamic_index_in_dim(solved, lax.axis_index("gx"), 0, keepdims=False)


def chain_constants(matrices, couples):
    return jnp.stack(
        [
            couples[0] * matrices[:, 0, 0],
            couples[0] * matrices[:, -1, 0],
            couples[1] * matrices[:, 0, -1],
            couples[1] * matrices[:, -1, -1],
        ]
    )


def line_apply(grouped, matrices, couples, known_groups):
    values = jnp.einsum("gic,cgm->igm", matrices, grouped, precision=PRECISE)
    group_count, column_count = (values.shape[1], values.shape[2])
    lower_couple = couples[0]
    upper_couple = couples[1]
    peers, rows_known = known_groups.shape[0], known_groups.shape[1]
    known = jnp.broadcast_to(
        known_groups[:, :, :, None], (peers, rows_known, group_count, column_count)
    ).reshape(peers, rows_known, group_count * column_count)
    chain_local = jnp.stack([values[0].reshape(-1), values[-1].reshape(-1)])
    solved = reduced_solve(chain_local, known)
    previous = solved[0].reshape(group_count, column_count)
    following = solved[1].reshape(group_count, column_count)
    first_column = jnp.transpose(matrices[:, :, 0])
    last_column = jnp.transpose(matrices[:, :, -1])
    return (
        values
        - (lower_couple[:, None] * previous)[None] * first_column[:, :, None]
        - (upper_couple[:, None] * following)[None] * last_column[:, :, None],
        previous,
        following,
    )


def row_apply(rows, matrix, couple_pair):
    values = jnp.einsum("mc,ic->mi", rows, matrix, precision=PRECISE)
    lower_couple = couple_pair[0]
    upper_couple = couple_pair[1]
    line_count = values.shape[0]

    def spread(value):
        return jnp.broadcast_to(value, (line_count,))

    chain_local = jnp.stack(
        [
            values[:, 0],
            values[:, -1],
            spread(lower_couple * matrix[0, 0]),
            spread(lower_couple * matrix[-1, 0]),
            spread(upper_couple * matrix[0, -1]),
            spread(upper_couple * matrix[-1, -1]),
        ]
    )
    solved = reduced_solve(chain_local)
    return (
        values
        - (lower_couple * solved[0])[:, None] * matrix[:, 0][None, :]
        - (upper_couple * solved[1])[:, None] * matrix[:, -1][None, :]
    )


def sorted_positions(layer_ids, layers, per_layer):
    depth_cells = layer_ids.shape[0]
    kinds = jnp.arange(layers, dtype=jnp.int32)
    onehot = (layer_ids[:, None] == kinds[None, :]).astype(jnp.int32)
    before = jnp.cumsum(onehot, axis=0) - onehot
    restore = jnp.sum(onehot * (before + kinds[None, :] * per_layer), axis=1)
    cells = jnp.arange(depth_cells, dtype=jnp.int32)
    order = jnp.sum(jnp.where(restore[None, :] == cells[:, None], cells[None, :], 0), axis=1)
    return order, restore


def local(
    source_field,
    permeability,
    layer_ids,
    inverse_fine,
    couple_fine,
    inverse_coarse,
    couple_coarse,
    owner_map,
):
    block_width, planes, depth_cells = source_field.shape
    layers = inverse_fine.shape[0]
    per_layer = depth_cells // layers
    order, restore = sorted_positions(layer_ids, layers, per_layer)
    halo_permeability = with_halo(permeability, (("gx", 0), ("gy", 1)), 1)
    face_list = face_terms(padded_depth(halo_permeability))
    rows = lax.axis_size("gy")
    up = [(i, i + 1) for i in range(rows - 1)]
    down = [(j, i) for i, j in up]

    def residual_of(field_now, left, right):
        lower = lax.ppermute(field_now[:, planes - 1 :, :], "gy", up)
        upper = lax.ppermute(field_now[:, :1, :], "gy", down)
        middle = jnp.concatenate([left, field_now, right], axis=0)
        padded = jnp.pad(middle, ((0, 0), (1, 1), (0, 0)))
        partial = source_field - apply_operator(padded_depth(padded), face_list)
        return (
            partial.at[:, :1, :]
            .add(face_list[2][:, :1, :] * lower)
            .at[:, planes - 1 :, :]
            .add(face_list[3][:, planes - 1 :, :] * upper)
        )

    def unsorted(lines):
        shaped = jnp.transpose(lines.reshape(layers, planes, per_layer), (1, 0, 2))
        return jnp.take(shaped.reshape(planes, depth_cells), restore, axis=1)[None]

    fine_couples = couple_fine[:, :, 0]
    fine_known = exchange(chain_constants(inverse_fine, fine_couples))
    solution = jnp.zeros_like(source_field)
    left = jnp.zeros_like(source_field[:1])
    right = jnp.zeros_like(source_field[:1])
    update = source_field
    for sweep_index in range(NSWEEP):
        if sweep_index > 0:
            update = residual_of(solution, left, right)
        ordered = jnp.take(update, order, axis=2).reshape(block_width, planes, layers, per_layer)
        change, previous, following = line_apply(
            jnp.transpose(ordered, (0, 2, 1, 3)).reshape(block_width, layers, planes * per_layer),
            inverse_fine,
            fine_couples,
            fine_known,
        )
        from_shaped = jnp.transpose(
            change.reshape(block_width, layers, planes, per_layer), (0, 2, 1, 3)
        )
        solution = solution + jnp.take(
            from_shaped.reshape(block_width, planes, depth_cells), restore, axis=2
        )
        left = left + unsorted(previous)
        right = right + unsorted(following)
    residual = residual_of(solution, left, right)
    coarse = 0.5 * (residual[:, 0::2, :] + residual[:, 1::2, :])
    groups = lax.axis_size("gy")
    position = lax.axis_index("gy")
    chunk = depth_cells // groups
    aggregates = 8
    owners = owner_map[:, 0]
    coarse_rows = jnp.take(jnp.transpose(coarse[:, 0, :]), order, axis=0)
    pieces = lax.all_to_all(
        coarse_rows.reshape(groups, chunk, block_width), "gy", 0, 0, tiled=True
    )
    member = (owners[:, None] == jnp.arange(aggregates, dtype=jnp.int32)[None, :]).astype(
        jnp.float32
    )
    summed = jnp.einsum("jzx,jo->ozx", pieces, member, precision=PRECISE)
    own_layer = (position * chunk) // per_layer
    matrix = lax.dynamic_index_in_dim(inverse_coarse, own_layer, 0, keepdims=False)
    couples = lax.dynamic_index_in_dim(couple_coarse[:, :, 0], own_layer, 1, keepdims=False)
    smoothed = row_apply(summed.reshape(aggregates * chunk, block_width), matrix, couples)
    outgoing = jnp.take(smoothed.reshape(aggregates, chunk, block_width), owners, axis=0)
    returned = lax.all_to_all(outgoing, "gy", 0, 0, tiled=True)
    result = jnp.take(returned.reshape(depth_cells, block_width), restore, axis=0)
    return (solution, residual, jnp.transpose(result)[:, None, :])


def solution(mesh):
    in_specs = (
        P("gx", "gy", None),
        P("gx", "gy", None),
        P(),
        P(None, "gx", None),
        P(None, None, "gx"),
        P(None, "gx", None),
        P(None, None, "gx"),
        P(),
    )
    out_specs = (P("gx", "gy", None), P("gx", "gy", None), P("gx", "gy", None))
    return jax.shard_map(local, mesh=mesh, in_specs=in_specs, out_specs=out_specs, check_vma=False)
```

```python
import jax
import jax.numpy as jnp
from jax import lax
from jax.sharding import PartitionSpec as P

NSWEEP = 3


PRECISE = lax.Precision.HIGHEST
WEIGHTS = (0.5, 0.5, 0.15, 0.15, 0.05, 0.05)
STORAGE = 0.1


def with_halo(array, sides, width):
    for axis, dim in sides:
        peers, length = (lax.axis_size(axis), array.shape[dim])
        up = [(i, (i + 1) % peers) for i in range(peers - 1)]
        down = [(j, i) for i, j in up]
        last = lax.slice_in_dim(array, length - width, length, axis=dim)
        leading = lax.slice_in_dim(array, 0, width, axis=dim)
        before = lax.ppermute(last, axis, up)
        after = lax.ppermute(leading, axis, down)
        array = jnp.concatenate([before, array, after], axis=dim)
    return array


def neighbours(padded):
    return [
        padded[:-2, 1:-1, 1:-1],
        padded[2:, 1:-1, 1:-1],
        padded[1:-1, :-2, 1:-1],
        padded[1:-1, 2:, 1:-1],
        padded[1:-1, 1:-1, :-2],
        padded[1:-1, 1:-1, 2:],
    ]


def face_terms(padded):
    centre = padded[1:-1, 1:-1, 1:-1]
    return [
        weight * 2.0 * centre * beside / (centre + beside)
        for weight, beside in zip(WEIGHTS, neighbours(padded))
    ]


def apply_operator(padded, face_list):
    centre = padded[1:-1, 1:-1, 1:-1]
    result_sum = STORAGE * centre
    for face_term, beside in zip(face_list, neighbours(padded)):
        result_sum = result_sum + face_term * (centre - beside)
    return result_sum


def padded_depth(field_now):
    return jnp.pad(field_now, ((0, 0), (0, 0), (1, 1)))


def chain_solve(chain_rows):
    blocks_count = chain_rows.shape[0]
    carry_value = jnp.zeros_like(chain_rows[0, 0])
    carry_gain = jnp.zeros_like(chain_rows[0, 0])
    first_parts, first_links, last_parts, last_links = ([], [], [], [])
    for block_index in range(blocks_count):
        pivot_value = 1.0 - chain_rows[block_index, 2] * carry_gain
        first_part = (
            chain_rows[block_index, 0] - chain_rows[block_index, 2] * carry_value
        ) / pivot_value
        first_link = chain_rows[block_index, 4] / pivot_value
        carry_value = (
            chain_rows[block_index, 1]
            - chain_rows[block_index, 3] * carry_value
            + chain_rows[block_index, 3] * carry_gain * first_part
        )
        carry_gain = (
            chain_rows[block_index, 5] + chain_rows[block_index, 3] * carry_gain * first_link
        )
        first_parts.append(first_part)
        first_links.append(first_link)
        last_parts.append(carry_value)
        last_links.append(carry_gain)
    following = jnp.zeros_like(carry_value)
    last_values = [following] * blocks_count
    next_values = [following] * blocks_count
    for block_index in range(blocks_count - 1, -1, -1):
        next_values[block_index] = following
        last_values[block_index] = last_parts[block_index] - last_links[block_index] * following
        following = first_parts[block_index] - first_links[block_index] * following
    previous = [jnp.zeros_like(following)] + last_values[:-1]
    return jnp.stack(
        [
            jnp.stack([previous[block_index], next_values[block_index]])
            for block_index in range(blocks_count)
        ]
    )


def reduced_solve(chain_local):
    peers = lax.axis_size("gx")
    packed = jnp.broadcast_to(chain_local[None], (peers,) + chain_local.shape)
    everyone = lax.all_to_all(packed, "gx", 0, 0, tiled=True)
    solved = chain_solve(everyone)
    return lax.dynamic_index_in_dim(solved, lax.axis_index("gx"), 0, keepdims=False)


def line_apply(grouped, matrices, couples):
    values = jnp.einsum("gic,cgm->igm", matrices, grouped, precision=PRECISE)
    group_count, column_count = (values.shape[1], values.shape[2])
    lower_couple = couples[0]
    upper_couple = couples[1]

    def spread(vector):
        return jnp.broadcast_to(vector[:, None], (group_count, column_count)).reshape(
            group_count * column_count
        )

    chain_local = jnp.stack(
        [
            values[0].reshape(-1),
            values[-1].reshape(-1),
            spread(lower_couple * matrices[:, 0, 0]),
            spread(lower_couple * matrices[:, -1, 0]),
            spread(upper_couple * matrices[:, 0, -1]),
            spread(upper_couple * matrices[:, -1, -1]),
        ]
    )
    solved = reduced_solve(chain_local)
    previous = solved[0].reshape(group_count, column_count)
    following = solved[1].reshape(group_count, column_count)
    first_column = jnp.transpose(matrices[:, :, 0])
    last_column = jnp.transpose(matrices[:, :, -1])
    return (
        values
        - (lower_couple[:, None] * previous)[None] * first_column[:, :, None]
        - (upper_couple[:, None] * following)[None] * last_column[:, :, None],
        previous,
        following,
    )


def row_apply(rows, matrix, couple_pair):
    values = jnp.einsum("mc,ic->mi", rows, matrix, precision=PRECISE)
    lower_couple = couple_pair[0]
    upper_couple = couple_pair[1]
    line_count = values.shape[0]

    def spread(value):
        return jnp.broadcast_to(value, (line_count,))

    chain_local = jnp.stack(
        [
            values[:, 0],
            values[:, -1],
            spread(lower_couple * matrix[0, 0]),
            spread(lower_couple * matrix[-1, 0]),
            spread(upper_couple * matrix[0, -1]),
            spread(upper_couple * matrix[-1, -1]),
        ]
    )
    solved = reduced_solve(chain_local)
    return (
        values
        - (lower_couple * solved[0])[:, None] * matrix[:, 0][None, :]
        - (upper_couple * solved[1])[:, None] * matrix[:, -1][None, :]
    )


def sorted_positions(layer_ids, layers, per_layer):
    depth_cells = layer_ids.shape[0]
    kinds = jnp.arange(layers, dtype=jnp.int32)
    onehot = (layer_ids[:, None] == kinds[None, :]).astype(jnp.int32)
    before = jnp.cumsum(onehot, axis=0) - onehot
    restore = jnp.sum(onehot * (before + kinds[None, :] * per_layer), axis=1)
    cells = jnp.arange(depth_cells, dtype=jnp.int32)
    order = jnp.sum(jnp.where(restore[None, :] == cells[:, None], cells[None, :], 0), axis=1)
    return order, restore


def local(
    source_field,
    permeability,
    layer_ids,
    inverse_fine,
    couple_fine,
    inverse_coarse,
    couple_coarse,
    owner_map,
):
    block_width, planes, depth_cells = source_field.shape
    layers = inverse_fine.shape[0]
    per_layer = depth_cells // layers
    order, restore = sorted_positions(layer_ids, layers, per_layer)
    halo_permeability = with_halo(permeability, (("gx", 0), ("gy", 1)), 1)
    face_list = face_terms(padded_depth(halo_permeability))
    rows = lax.axis_size("gy")
    up = [(i, i + 1) for i in range(rows - 1)]
    down = [(j, i) for i, j in up]

    def residual_of(field_now, left, right):
        lower = lax.ppermute(field_now[:, planes - 1 :, :], "gy", up)
        upper = lax.ppermute(field_now[:, :1, :], "gy", down)
        middle = jnp.concatenate([left, field_now, right], axis=0)
        padded = jnp.pad(middle, ((0, 0), (1, 1), (0, 0)))
        partial = source_field - apply_operator(padded_depth(padded), face_list)
        return (
            partial.at[:, :1, :]
            .add(face_list[2][:, :1, :] * lower)
            .at[:, planes - 1 :, :]
            .add(face_list[3][:, planes - 1 :, :] * upper)
        )

    def unsorted(lines):
        shaped = jnp.transpose(lines.reshape(layers, planes, per_layer), (1, 0, 2))
        return jnp.take(shaped.reshape(planes, depth_cells), restore, axis=1, mode="clip")[None]

    fine_couples = couple_fine[:, :, 0]
    solution = jnp.zeros_like(source_field)
    left = jnp.zeros_like(source_field[:1])
    right = jnp.zeros_like(source_field[:1])
    update = source_field
    for sweep_index in range(NSWEEP):
        if sweep_index > 0:
            update = residual_of(solution, left, right)
        ordered = jnp.take(update, order, axis=2, mode="clip").reshape(block_width, planes, layers, per_layer)
        change, previous, following = line_apply(
            jnp.transpose(ordered, (0, 2, 1, 3)).reshape(block_width, layers, planes * per_layer),
            inverse_fine,
            fine_couples,
        )
        from_shaped = jnp.transpose(
            change.reshape(block_width, layers, planes, per_layer), (0, 2, 1, 3)
        )
        solution = solution + jnp.take(
            from_shaped.reshape(block_width, planes, depth_cells), restore, axis=2
        , mode="clip")
        left = left + unsorted(previous)
        right = right + unsorted(following)
    residual = residual_of(solution, left, right)
    coarse = 0.5 * (residual[:, 0::2, :] + residual[:, 1::2, :])
    groups = lax.axis_size("gy")
    position = lax.axis_index("gy")
    chunk = depth_cells // groups
    aggregates = 8
    owners = owner_map[:, 0]
    coarse_rows = jnp.take(jnp.transpose(coarse[:, 0, :]), order, axis=0, mode="clip")
    pieces = lax.all_to_all(
        coarse_rows.reshape(groups, chunk, block_width), "gy", 0, 0, tiled=True
    )
    member = (owners[:, None] == jnp.arange(aggregates, dtype=jnp.int32)[None, :]).astype(
        jnp.float32
    )
    summed = jnp.einsum("jzx,jo->ozx", pieces, member, precision=PRECISE)
    own_layer = (position * chunk) // per_layer
    matrix = lax.dynamic_index_in_dim(inverse_coarse, own_layer, 0, keepdims=False)
    couples = lax.dynamic_index_in_dim(couple_coarse[:, :, 0], own_layer, 1, keepdims=False)
    smoothed = row_apply(summed.reshape(aggregates * chunk, block_width), matrix, couples)
    outgoing = jnp.take(smoothed.reshape(aggregates, chunk, block_width), owners, axis=0, mode="clip")
    returned = lax.all_to_all(outgoing, "gy", 0, 0, tiled=True)
    result = jnp.take(returned.reshape(depth_cells, block_width), restore, axis=0, mode="clip")
    return (solution, residual, jnp.transpose(result)[:, None, :])


def solution(mesh):
    in_specs = (
        P("gx", "gy", None),
        P("gx", "gy", None),
        P(),
        P(None, "gx", None),
        P(None, None, "gx"),
        P(None, "gx", None),
        P(None, None, "gx"),
        P(),
    )
    out_specs = (P("gx", "gy", None), P("gx", "gy", None), P("gx", "gy", None))
    return jax.shard_map(local, mesh=mesh, in_specs=in_specs, out_specs=out_specs, check_vma=False)
```

```python
import jax
import jax.numpy as jnp
from jax import lax
from jax.sharding import PartitionSpec as P

NSWEEP = 3


PRECISE = lax.Precision.HIGHEST
WEIGHTS = (0.5, 0.5, 0.15, 0.15, 0.05, 0.05)
STORAGE = 0.1


def with_halo(array, sides, width):
    for axis, dim in sides:
        peers, length = (lax.axis_size(axis), array.shape[dim])
        up = [(i, (i + 1) % peers) for i in range(peers - 1)]
        down = [(j, i) for i, j in up]
        last = lax.slice_in_dim(array, length - width, length, axis=dim)
        leading = lax.slice_in_dim(array, 0, width, axis=dim)
        before = lax.ppermute(last, axis, up)
        after = lax.ppermute(leading, axis, down)
        array = jnp.concatenate([before, array, after], axis=dim)
    return array


def neighbours(padded):
    return [
        padded[:-2, 1:-1, 1:-1],
        padded[2:, 1:-1, 1:-1],
        padded[1:-1, :-2, 1:-1],
        padded[1:-1, 2:, 1:-1],
        padded[1:-1, 1:-1, :-2],
        padded[1:-1, 1:-1, 2:],
    ]


def face_terms(padded):
    centre = padded[1:-1, 1:-1, 1:-1]
    return [
        weight * 2.0 * centre * beside / (centre + beside)
        for weight, beside in zip(WEIGHTS, neighbours(padded))
    ]


def apply_operator(padded, face_list):
    centre = padded[1:-1, 1:-1, 1:-1]
    result_sum = STORAGE * centre
    for face_term, beside in zip(face_list, neighbours(padded)):
        result_sum = result_sum + face_term * (centre - beside)
    return result_sum


def padded_depth(field_now):
    return jnp.pad(field_now, ((0, 0), (0, 0), (1, 1)))


def chain_solve(chain_rows):
    blocks_count = chain_rows.shape[0]
    carry_value = jnp.zeros_like(chain_rows[0, 0])
    carry_gain = jnp.zeros_like(chain_rows[0, 0])
    first_parts, first_links, last_parts, last_links = ([], [], [], [])
    for block_index in range(blocks_count):
        pivot_value = 1.0 - chain_rows[block_index, 2] * carry_gain
        first_part = (
            chain_rows[block_index, 0] - chain_rows[block_index, 2] * carry_value
        ) / pivot_value
        first_link = chain_rows[block_index, 4] / pivot_value
        carry_value = (
            chain_rows[block_index, 1]
            - chain_rows[block_index, 3] * carry_value
            + chain_rows[block_index, 3] * carry_gain * first_part
        )
        carry_gain = (
            chain_rows[block_index, 5] + chain_rows[block_index, 3] * carry_gain * first_link
        )
        first_parts.append(first_part)
        first_links.append(first_link)
        last_parts.append(carry_value)
        last_links.append(carry_gain)
    following = jnp.zeros_like(carry_value)
    last_values = [following] * blocks_count
    next_values = [following] * blocks_count
    for block_index in range(blocks_count - 1, -1, -1):
        next_values[block_index] = following
        last_values[block_index] = last_parts[block_index] - last_links[block_index] * following
        following = first_parts[block_index] - first_links[block_index] * following
    previous = [jnp.zeros_like(following)] + last_values[:-1]
    return jnp.stack(
        [
            jnp.stack([previous[block_index], next_values[block_index]])
            for block_index in range(blocks_count)
        ]
    )


def reduced_solve(chain_local):
    peers = lax.axis_size("gx")
    packed = jnp.broadcast_to(chain_local[None], (peers,) + chain_local.shape)
    everyone = lax.all_to_all(packed, "gx", 0, 0, tiled=True)
    solved = chain_solve(everyone)
    return lax.dynamic_index_in_dim(solved, lax.axis_index("gx"), 0, keepdims=False)


def line_apply(grouped, matrices, couples):
    values = jnp.einsum("gic,cgm->igm", matrices, grouped, precision=PRECISE)
    group_count, column_count = (values.shape[1], values.shape[2])
    lower_couple = couples[0]
    upper_couple = couples[1]

    def spread(vector):
        return jnp.broadcast_to(vector[:, None], (group_count, column_count)).reshape(
            group_count * column_count
        )

    chain_local = jnp.stack(
        [
            values[0].reshape(-1),
            values[-1].reshape(-1),
            spread(lower_couple * matrices[:, 0, 0]),
            spread(lower_couple * matrices[:, -1, 0]),
            spread(upper_couple * matrices[:, 0, -1]),
            spread(upper_couple * matrices[:, -1, -1]),
        ]
    )
    solved = reduced_solve(chain_local)
    previous = solved[0].reshape(group_count, column_count)
    following = solved[1].reshape(group_count, column_count)
    first_column = jnp.transpose(matrices[:, :, 0])
    last_column = jnp.transpose(matrices[:, :, -1])
    return (
        values
        - (lower_couple[:, None] * previous)[None] * first_column[:, :, None]
        - (upper_couple[:, None] * following)[None] * last_column[:, :, None],
        previous,
        following,
    )


def row_apply(rows, matrix, couple_pair):
    values = jnp.einsum("mc,ic->mi", rows, matrix, precision=PRECISE)
    lower_couple = couple_pair[0]
    upper_couple = couple_pair[1]
    line_count = values.shape[0]

    def spread(value):
        return jnp.broadcast_to(value, (line_count,))

    chain_local = jnp.stack(
        [
            values[:, 0],
            values[:, -1],
            spread(lower_couple * matrix[0, 0]),
            spread(lower_couple * matrix[-1, 0]),
            spread(upper_couple * matrix[0, -1]),
            spread(upper_couple * matrix[-1, -1]),
        ]
    )
    solved = reduced_solve(chain_local)
    return (
        values
        - (lower_couple * solved[0])[:, None] * matrix[:, 0][None, :]
        - (upper_couple * solved[1])[:, None] * matrix[:, -1][None, :]
    )


def sorted_positions(layer_ids, layers, per_layer):
    depth_cells = layer_ids.shape[0]
    kinds = jnp.arange(layers, dtype=jnp.int32)
    onehot = (layer_ids[:, None] == kinds[None, :]).astype(jnp.int32)
    before = jnp.cumsum(onehot, axis=0) - onehot
    restore = jnp.sum(onehot * (before + kinds[None, :] * per_layer), axis=1)
    cells = jnp.arange(depth_cells, dtype=jnp.int32)
    order = jnp.sum(jnp.where(restore[None, :] == cells[:, None], cells[None, :], 0), axis=1)
    return order, restore


def local(
    source_field,
    permeability,
    layer_ids,
    inverse_fine,
    couple_fine,
    inverse_coarse,
    couple_coarse,
    owner_map,
):
    block_width, planes, depth_cells = source_field.shape
    layers = inverse_fine.shape[0]
    per_layer = depth_cells // layers
    order, restore = sorted_positions(layer_ids, layers, per_layer)
    rows = lax.axis_size("gy")
    up = [(i, i + 1) for i in range(rows - 1)]
    down = [(j, i) for i, j in up]
    across = with_halo(permeability, (("gx", 0),), 1)
    below = lax.ppermute(permeability[:, planes - 1 :, :], "gy", up)
    above = lax.ppermute(permeability[:, :1, :], "gy", down)
    rim = ((1, 1), (0, 0), (0, 0))
    halo_permeability = jnp.concatenate([jnp.pad(below, rim), across, jnp.pad(above, rim)], axis=1)
    face_list = face_terms(padded_depth(halo_permeability))

    def residual_of(field_now, left, right):
        lower = lax.ppermute(field_now[:, planes - 1 :, :], "gy", up)
        upper = lax.ppermute(field_now[:, :1, :], "gy", down)
        middle = jnp.concatenate([left, field_now, right], axis=0)
        padded = jnp.pad(middle, ((0, 0), (1, 1), (0, 0)))
        partial = source_field - apply_operator(padded_depth(padded), face_list)
        return (
            partial.at[:, :1, :]
            .add(face_list[2][:, :1, :] * lower)
            .at[:, planes - 1 :, :]
            .add(face_list[3][:, planes - 1 :, :] * upper)
        )

    def unsorted(lines):
        shaped = jnp.transpose(lines.reshape(layers, planes, per_layer), (1, 0, 2))
        return jnp.take(shaped.reshape(planes, depth_cells), restore, axis=1, mode="clip")[None]

    fine_couples = couple_fine[:, :, 0]
    solution = jnp.zeros_like(source_field)
    left = jnp.zeros_like(source_field[:1])
    right = jnp.zeros_like(source_field[:1])
    update = source_field
    for sweep_index in range(NSWEEP):
        if sweep_index > 0:
            update = residual_of(solution, left, right)
        ordered = jnp.take(update, order, axis=2, mode="clip").reshape(block_width, planes, layers, per_layer)
        change, previous, following = line_apply(
            jnp.transpose(ordered, (0, 2, 1, 3)).reshape(block_width, layers, planes * per_layer),
            inverse_fine,
            fine_couples,
        )
        from_shaped = jnp.transpose(
            change.reshape(block_width, layers, planes, per_layer), (0, 2, 1, 3)
        )
        solution = solution + jnp.take(
            from_shaped.reshape(block_width, planes, depth_cells), restore, axis=2
        , mode="clip")
        left = left + unsorted(previous)
        right = right + unsorted(following)
    residual = residual_of(solution, left, right)
    coarse = 0.5 * (residual[:, 0::2, :] + residual[:, 1::2, :])
    groups = lax.axis_size("gy")
    position = lax.axis_index("gy")
    chunk = depth_cells // groups
    aggregates = 8
    owners = owner_map[:, 0]
    coarse_rows = jnp.take(jnp.transpose(coarse[:, 0, :]), order, axis=0, mode="clip")
    pieces = lax.all_to_all(
        coarse_rows.reshape(groups, chunk, block_width), "gy", 0, 0, tiled=True
    )
    member = (owners[:, None] == jnp.arange(aggregates, dtype=jnp.int32)[None, :]).astype(
        jnp.float32
    )
    summed = jnp.einsum("jzx,jo->ozx", pieces, member, precision=PRECISE)
    own_layer = (position * chunk) // per_layer
    matrix = lax.dynamic_index_in_dim(inverse_coarse, own_layer, 0, keepdims=False)
    couples = lax.dynamic_index_in_dim(couple_coarse[:, :, 0], own_layer, 1, keepdims=False)
    smoothed = row_apply(summed.reshape(aggregates * chunk, block_width), matrix, couples)
    outgoing = jnp.take(smoothed.reshape(aggregates, chunk, block_width), owners, axis=0, mode="clip")
    returned = lax.all_to_all(outgoing, "gy", 0, 0, tiled=True)
    result = jnp.take(returned.reshape(depth_cells, block_width), restore, axis=0, mode="clip")
    return (solution, residual, jnp.transpose(result)[:, None, :])


def solution(mesh):
    in_specs = (
        P("gx", "gy", None),
        P("gx", "gy", None),
        P(),
        P(None, "gx", None),
        P(None, None, "gx"),
        P(None, "gx", None),
        P(None, None, "gx"),
        P(),
    )
    out_specs = (P("gx", "gy", None), P("gx", "gy", None), P("gx", "gy", None))
    return jax.shard_map(local, mesh=mesh, in_specs=in_specs, out_specs=out_specs, check_vma=False)
```

```python
import jax
import jax.numpy as jnp
from jax import lax
from jax.sharding import PartitionSpec as P

NSWEEP = 3


PRECISE = lax.Precision.HIGHEST
WEIGHTS = (0.5, 0.5, 0.15, 0.15, 0.05, 0.05)
STORAGE = 0.1


def with_halo(array, sides, width):
    for axis, dim in sides:
        peers, length = (lax.axis_size(axis), array.shape[dim])
        up = [(i, (i + 1) % peers) for i in range(peers - 1)]
        down = [(j, i) for i, j in up]
        last = lax.slice_in_dim(array, length - width, length, axis=dim)
        leading = lax.slice_in_dim(array, 0, width, axis=dim)
        before = lax.ppermute(last, axis, up)
        after = lax.ppermute(leading, axis, down)
        array = jnp.concatenate([before, array, after], axis=dim)
    return array


def neighbours(padded):
    return [
        padded[:-2, 1:-1, 1:-1],
        padded[2:, 1:-1, 1:-1],
        padded[1:-1, :-2, 1:-1],
        padded[1:-1, 2:, 1:-1],
        padded[1:-1, 1:-1, :-2],
        padded[1:-1, 1:-1, 2:],
    ]


def face_terms(padded):
    centre = padded[1:-1, 1:-1, 1:-1]
    return [
        weight * 2.0 * centre * beside / (centre + beside)
        for weight, beside in zip(WEIGHTS, neighbours(padded))
    ]


def apply_operator(padded, face_list):
    centre = padded[1:-1, 1:-1, 1:-1]
    result_sum = STORAGE * centre
    for face_term, beside in zip(face_list, neighbours(padded)):
        result_sum = result_sum + face_term * (centre - beside)
    return result_sum


def padded_depth(field_now):
    return jnp.pad(field_now, ((0, 0), (0, 0), (1, 1)))


def chain_solve(chain_rows):
    blocks_count = chain_rows.shape[0]
    carry_value = jnp.zeros_like(chain_rows[0, 0])
    carry_gain = jnp.zeros_like(chain_rows[0, 0])
    first_parts, first_links, last_parts, last_links = ([], [], [], [])
    for block_index in range(blocks_count):
        pivot_value = 1.0 - chain_rows[block_index, 2] * carry_gain
        first_part = (
            chain_rows[block_index, 0] - chain_rows[block_index, 2] * carry_value
        ) / pivot_value
        first_link = chain_rows[block_index, 4] / pivot_value
        carry_value = (
            chain_rows[block_index, 1]
            - chain_rows[block_index, 3] * carry_value
            + chain_rows[block_index, 3] * carry_gain * first_part
        )
        carry_gain = (
            chain_rows[block_index, 5] + chain_rows[block_index, 3] * carry_gain * first_link
        )
        first_parts.append(first_part)
        first_links.append(first_link)
        last_parts.append(carry_value)
        last_links.append(carry_gain)
    following = jnp.zeros_like(carry_value)
    last_values = [following] * blocks_count
    next_values = [following] * blocks_count
    for block_index in range(blocks_count - 1, -1, -1):
        next_values[block_index] = following
        last_values[block_index] = last_parts[block_index] - last_links[block_index] * following
        following = first_parts[block_index] - first_links[block_index] * following
    previous = [jnp.zeros_like(following)] + last_values[:-1]
    return jnp.stack(
        [
            jnp.stack([previous[block_index], next_values[block_index]])
            for block_index in range(blocks_count)
        ]
    )


def reduced_solve(chain_local, extra=None):
    peers = lax.axis_size("gx")
    rows = chain_local.shape[0]
    if extra is not None:
        chain_local = jnp.concatenate([chain_local, extra], axis=0)
    packed = jnp.broadcast_to(chain_local[None], (peers,) + chain_local.shape)
    everyone = lax.all_to_all(packed, "gx", 0, 0, tiled=True)
    solved = chain_solve(everyone[:, :rows])
    own = lax.dynamic_index_in_dim(solved, lax.axis_index("gx"), 0, keepdims=False)
    if extra is None:
        return own
    return own, everyone[:, rows:]


def line_apply(grouped, matrices, couples, extra=None):
    values = jnp.einsum("gic,cgm->igm", matrices, grouped, precision=PRECISE)
    group_count, column_count = (values.shape[1], values.shape[2])
    lower_couple = couples[0]
    upper_couple = couples[1]

    def spread(vector):
        return jnp.broadcast_to(vector[:, None], (group_count, column_count)).reshape(
            group_count * column_count
        )

    chain_local = jnp.stack(
        [
            values[0].reshape(-1),
            values[-1].reshape(-1),
            spread(lower_couple * matrices[:, 0, 0]),
            spread(lower_couple * matrices[:, -1, 0]),
            spread(upper_couple * matrices[:, 0, -1]),
            spread(upper_couple * matrices[:, -1, -1]),
        ]
    )
    solved = reduced_solve(chain_local, extra)
    if extra is not None:
        solved, carried = solved
    previous = solved[0].reshape(group_count, column_count)
    following = solved[1].reshape(group_count, column_count)
    first_column = jnp.transpose(matrices[:, :, 0])
    last_column = jnp.transpose(matrices[:, :, -1])
    return (
        values
        - (lower_couple[:, None] * previous)[None] * first_column[:, :, None]
        - (upper_couple[:, None] * following)[None] * last_column[:, :, None],
        previous,
        following,
    ) + ((carried,) if extra is not None else ())


def row_apply(rows, matrix, couple_pair):
    values = jnp.einsum("mc,ic->mi", rows, matrix, precision=PRECISE)
    lower_couple = couple_pair[0]
    upper_couple = couple_pair[1]
    line_count = values.shape[0]

    def spread(value):
        return jnp.broadcast_to(value, (line_count,))

    chain_local = jnp.stack(
        [
            values[:, 0],
            values[:, -1],
            spread(lower_couple * matrix[0, 0]),
            spread(lower_couple * matrix[-1, 0]),
            spread(upper_couple * matrix[0, -1]),
            spread(upper_couple * matrix[-1, -1]),
        ]
    )
    solved = reduced_solve(chain_local)
    return (
        values
        - (lower_couple * solved[0])[:, None] * matrix[:, 0][None, :]
        - (upper_couple * solved[1])[:, None] * matrix[:, -1][None, :]
    )


def sorted_positions(layer_ids, layers, per_layer):
    depth_cells = layer_ids.shape[0]
    kinds = jnp.arange(layers, dtype=jnp.int32)
    onehot = (layer_ids[:, None] == kinds[None, :]).astype(jnp.int32)
    before = jnp.cumsum(onehot, axis=0) - onehot
    restore = jnp.sum(onehot * (before + kinds[None, :] * per_layer), axis=1)
    cells = jnp.arange(depth_cells, dtype=jnp.int32)
    order = jnp.sum(jnp.where(restore[None, :] == cells[:, None], cells[None, :], 0), axis=1)
    return order, restore


def local(
    source_field,
    permeability,
    layer_ids,
    inverse_fine,
    couple_fine,
    inverse_coarse,
    couple_coarse,
    owner_map,
):
    block_width, planes, depth_cells = source_field.shape
    layers = inverse_fine.shape[0]
    per_layer = depth_cells // layers
    order, restore = sorted_positions(layer_ids, layers, per_layer)
    rows = lax.axis_size("gy")
    up = [(i, i + 1) for i in range(rows - 1)]
    down = [(j, i) for i, j in up]
    below = lax.ppermute(permeability[:, planes - 1 :, :], "gy", up)
    above = lax.ppermute(permeability[:, :1, :], "gy", down)
    rim = ((1, 1), (0, 0), (0, 0))
    ends = jnp.stack([permeability[0].reshape(-1), permeability[-1].reshape(-1)])
    face_list = None

    def faces_from(carried):
        peers = lax.axis_size("gx")
        here = lax.axis_index("gx")
        left_block = lax.dynamic_index_in_dim(carried, jnp.maximum(here - 1, 0), 0, keepdims=False)
        right_block = lax.dynamic_index_in_dim(
            carried, jnp.minimum(here + 1, peers - 1), 0, keepdims=False
        )
        left_k = jnp.where(here > 0, left_block[1], 0.0).reshape(1, planes, depth_cells)
        right_k = jnp.where(here < peers - 1, right_block[0], 0.0).reshape(1, planes, depth_cells)
        across = jnp.concatenate([left_k, permeability, right_k], axis=0)
        halo = jnp.concatenate([jnp.pad(below, rim), across, jnp.pad(above, rim)], axis=1)
        return face_terms(padded_depth(halo))

    def residual_of(field_now, left, right, face_list):
        lower = lax.ppermute(field_now[:, planes - 1 :, :], "gy", up)
        upper = lax.ppermute(field_now[:, :1, :], "gy", down)
        middle = jnp.concatenate([left, field_now, right], axis=0)
        padded = jnp.pad(middle, ((0, 0), (1, 1), (0, 0)))
        partial = source_field - apply_operator(padded_depth(padded), face_list)
        return (
            partial.at[:, :1, :]
            .add(face_list[2][:, :1, :] * lower)
            .at[:, planes - 1 :, :]
            .add(face_list[3][:, planes - 1 :, :] * upper)
        )

    def unsorted(lines):
        shaped = jnp.transpose(lines.reshape(layers, planes, per_layer), (1, 0, 2))
        return jnp.take(shaped.reshape(planes, depth_cells), restore, axis=1, mode="clip")[None]

    fine_couples = couple_fine[:, :, 0]
    solution = jnp.zeros_like(source_field)
    left = jnp.zeros_like(source_field[:1])
    right = jnp.zeros_like(source_field[:1])
    update = source_field
    for sweep_index in range(NSWEEP):
        if sweep_index > 0:
            update = residual_of(solution, left, right, face_list)
        ordered = jnp.take(update, order, axis=2, mode="clip").reshape(block_width, planes, layers, per_layer)
        outputs = line_apply(
            jnp.transpose(ordered, (0, 2, 1, 3)).reshape(block_width, layers, planes * per_layer),
            inverse_fine,
            fine_couples,
            ends if face_list is None else None,
        )
        change, previous, following = outputs[:3]
        if face_list is None:
            face_list = faces_from(outputs[3])
        from_shaped = jnp.transpose(
            change.reshape(block_width, layers, planes, per_layer), (0, 2, 1, 3)
        )
        solution = solution + jnp.take(
            from_shaped.reshape(block_width, planes, depth_cells), restore, axis=2
        , mode="clip")
        left = left + unsorted(previous)
        right = right + unsorted(following)
    residual = residual_of(solution, left, right, face_list)
    coarse = 0.5 * (residual[:, 0::2, :] + residual[:, 1::2, :])
    groups = lax.axis_size("gy")
    position = lax.axis_index("gy")
    chunk = depth_cells // groups
    aggregates = 8
    owners = owner_map[:, 0]
    coarse_rows = jnp.take(jnp.transpose(coarse[:, 0, :]), order, axis=0, mode="clip")
    pieces = lax.all_to_all(
        coarse_rows.reshape(groups, chunk, block_width), "gy", 0, 0, tiled=True
    )
    member = (owners[:, None] == jnp.arange(aggregates, dtype=jnp.int32)[None, :]).astype(
        jnp.float32
    )
    summed = jnp.einsum("jzx,jo->ozx", pieces, member, precision=PRECISE)
    own_layer = (position * chunk) // per_layer
    matrix = lax.dynamic_index_in_dim(inverse_coarse, own_layer, 0, keepdims=False)
    couples = lax.dynamic_index_in_dim(couple_coarse[:, :, 0], own_layer, 1, keepdims=False)
    smoothed = row_apply(summed.reshape(aggregates * chunk, block_width), matrix, couples)
    outgoing = jnp.take(smoothed.reshape(aggregates, chunk, block_width), owners, axis=0, mode="clip")
    returned = lax.all_to_all(outgoing, "gy", 0, 0, tiled=True)
    result = jnp.take(returned.reshape(depth_cells, block_width), restore, axis=0, mode="clip")
    return (solution, residual, jnp.transpose(result)[:, None, :])


def solution(mesh):
    in_specs = (
        P("gx", "gy", None),
        P("gx", "gy", None),
        P(),
        P(None, "gx", None),
        P(None, None, "gx"),
        P(None, "gx", None),
        P(None, None, "gx"),
        P(),
    )
    out_specs = (P("gx", "gy", None), P("gx", "gy", None), P("gx", "gy", None))
    return jax.shard_map(local, mesh=mesh, in_specs=in_specs, out_specs=out_specs, check_vma=False)
```
